32 devices in a mesh: gx: 16 (over z, y, x), gy: 2 (over core).
Axes of the slice: x: 2, y: 2, z: 4, core: 2. Of those that a mesh axis runs over, the one named last changes fastest.
Arguments:
- load_parts: bfloat16 [16, 2, 4, 192, 384], P('gx', 'gy'), may hold values from -6 to 6
- schur: bfloat16 [16, 2, 4, 384, 384], P('gx', 'gy'), may hold values from -4 to 4
- deluxe: bfloat16 [16, 2, 4, 384, 384], P('gx', 'gy'), may hold values from -4 to 4
- panels: bfloat16 [16, 2, 4, 384, 384], P('gx', 'gy'), may hold values from -4 to 4
- coarse_inverse: float32 [128, 128], P(('gx', 'gy')), may hold values from -1 to 1
- primal_dofs: int32 [16, 2, 4], P('gx', 'gy'), may hold values from 0 to 1535
- damage_flags: int32 [16, 2, 4], P('gx', 'gy'), may hold values 0 or 1
Outputs:
- increment: bfloat16 [16, 2, 4, 192, 384], P('gx', 'gy')
The draws below stay inside these ranges and needn't reach their ends.
Inputs may be any that keep to these rules, and one draw needn't show every extreme that they name: `primal_dofs`: each entry names a face times 384 plus a position on that face.
All inputs are finite; a program needn't handle non-finite values. No bound on the sum of `damage_flags` on one device may be relied on, other than what follows from the above.
Results may differ from the reference program's by a relative error of at most 0.003.
The reference program's roundings to bfloat16 on the way (of `neighbour`, `scaled`, `primal`, `weighted` and `spread`) count: a program that leaves them out, or rounds other values in their place, can miss the bound.
Values may be sent and summed in bfloat16 or wider, within the bound.
No kernel may reach another device: no remote copies, remote signals or barrier semaphores. Data moves between devices by JAX's collectives and lax.ppermute only.
A program may use at most 64 MiB of HBM per device.

```python
import math
import jax
import jax.numpy as jnp
from jax import lax

FACE_DOFS = 384
LOADS = 192
PRIMAL = 4
SUB_X = 16
SUB_Y = 2
COARSE = 128


def dominant_panel(key, diag, off, symmetric):
    key_base, key_diag = jax.random.split(key)
    shape = (SUB_X, SUB_Y, 4, FACE_DOFS, FACE_DOFS)
    base = jax.random.truncated_normal(key_base, -3.0, 3.0, shape, jnp.float32)
    base = base * (off / math.sqrt(FACE_DOFS))
    if symmetric:
        base = (base + jnp.swapaxes(base, -1, -2)) * 0.7071
    scales = jax.random.uniform(key_diag, (SUB_X, SUB_Y, 4, FACE_DOFS), jnp.float32, 0.7, 1.3) * diag
    identity = jnp.eye(FACE_DOFS, dtype=jnp.float32)
    return base + identity * scales[:, :, :, None, :]


def draw_schur(key, part):
    return dominant_panel(jax.random.fold_in(key, 11), 2.5, 0.6, True).astype(jnp.bfloat16)


def draw_deluxe(key, part):
    return dominant_panel(jax.random.fold_in(key, 23), 0.6, 0.25, False).astype(jnp.bfloat16)


def draw_panels(key, part):
    return dominant_panel(jax.random.fold_in(key, 37), 1.0, 0.4, False).astype(jnp.bfloat16)


def touch_ends(result, stream_key, low, top_value):
    extent = result.shape
    spot = [jax.random.randint(jax.random.fold_in(stream_key, axis), (), 0, extent[axis]) for axis in range(len(extent))]
    result = result.at[tuple(spot)].set(low)
    longest = extent.index(max(extent))
    spot[longest] = (spot[longest] + 1) % extent[longest]
    return result.at[tuple(spot)].set(top_value)


def block_scale(own_key, dims, shards, smallest, high):
    level = 1.0
    for position, shards_of in shards:
        heights = jax.random.uniform(jax.random.fold_in(jax.random.fold_in(own_key, 6), position), (shards_of,), jnp.float32, smallest / len(shards), high / len(shards))
        level = level * jnp.repeat(jnp.exp(heights), dims[position] // shards_of).reshape((-1,) + (1,) * (len(dims) - 1 - position))
    return level


def scatter_about(stream_key, dims, deviation, limit, shards=(), held_as=jnp.bfloat16):
    entries = jax.random.normal(stream_key, dims, jnp.float32) * deviation
    if len(shards) > 0:
        entries = block_scale(stream_key, dims, shards, -0.22, 0.18) * entries
    return jnp.clip(entries, min=-limit, max=limit).astype(held_as)


def setup_inputs(seed: int = 0) -> dict:
    splits = jax.random.split(jax.random.key(seed), 8)
    return {
        "load_parts": scatter_about(splits[0], (SUB_X, SUB_Y, 4, LOADS, FACE_DOFS), 1.0, 6.0, ((0, 16), (1, 2))),
        "schur": draw_schur(jax.random.fold_in(splits[7], 71), 0),
        "deluxe": draw_deluxe(jax.random.fold_in(splits[7], 71), 0),
        "panels": draw_panels(jax.random.fold_in(splits[7], 71), 0),
        "coarse_inverse": scatter_about(splits[4], (COARSE, COARSE), (COARSE // 4) ** -0.5, 1.0, ((0, 32),), jnp.float32),
        "primal_dofs": touch_ends(jax.random.randint(splits[5], (SUB_X, SUB_Y, PRIMAL), 0, 4 * FACE_DOFS), jax.random.fold_in(splits[5], 1), 0, (4 * FACE_DOFS) - 1).astype(jnp.int32),
        "damage_flags": touch_ends((jax.random.randint(splits[6], (SUB_X, SUB_Y, 4), 0, 3) < 1).astype(jnp.int32), jax.random.fold_in(splits[6], 1), 0, 1),
    }


def neighbour(values):
    zero_x = jnp.zeros_like(values[:1, :, 0])
    first = jnp.concatenate([zero_x, values[:-1, :, 1]], axis=0)
    second = jnp.concatenate([values[1:, :, 0], zero_x], axis=0)
    zero_y = jnp.zeros_like(values[:, :1, 2])
    third = jnp.concatenate([zero_y, values[:, :-1, 3]], axis=1)
    fourth = jnp.concatenate([values[:, 1:, 2], zero_y], axis=1)
    return jnp.stack([first, second, third, fourth], axis=2)


def face_product(vectors, matrices, form):
    def one_row(pair):
        return jnp.einsum(form, pair[0].astype(jnp.float32), pair[1].astype(jnp.float32))
    return lax.map(one_row, (vectors, matrices))


def precondition(resid, deluxe, panels, coarse_inverse, selector, flags):
    scaled = face_product(resid.astype(jnp.bfloat16), deluxe, "bfry,bfxy->bfrx").astype(jnp.bfloat16)
    local_part = face_product(scaled, panels, "bfry,bfyx->bfrx")
    extra = face_product(local_part.astype(jnp.bfloat16), panels, "bfry,bfyx->bfrx")
    softened = local_part + 0.5 * flags[:, :, :, None, None] * extra
    primal = jnp.einsum("abkfx,abfrx->abkr", selector, scaled.astype(jnp.float32)).astype(jnp.bfloat16)
    flat = primal.reshape(COARSE, LOADS).astype(jnp.float32)
    coarse = jnp.dot(coarse_inverse, flat, precision=lax.Precision.HIGHEST).reshape(SUB_X, SUB_Y, PRIMAL, LOADS)
    placed = jnp.einsum("abkfx,abkr->abfrx", selector, coarse, precision=lax.Precision.HIGHEST)
    weighted = (softened + placed).astype(jnp.bfloat16)
    spread = face_product(weighted, deluxe, "bfry,bfyx->bfrx").astype(jnp.bfloat16)
    return spread.astype(jnp.float32) + neighbour(spread).astype(jnp.float32)


def operator(field, schur):
    bent = face_product(field.astype(jnp.bfloat16), schur, "bfry,bfyx->bfrx").astype(jnp.bfloat16)
    return bent.astype(jnp.float32) + neighbour(bent).astype(jnp.float32)


def reference(load_parts, schur, deluxe, panels, coarse_inverse, primal_dofs, damage_flags):
    resid0 = load_parts.astype(jnp.float32) + neighbour(load_parts).astype(jnp.float32)
    positions = jnp.arange(4 * FACE_DOFS, dtype=jnp.int32)
    selector = (primal_dofs[:, :, :, None] == positions).astype(jnp.float32)
    selector = selector.reshape(SUB_X, SUB_Y, PRIMAL, 4, FACE_DOFS)
    flags = damage_flags.astype(jnp.float32)
    first = precondition(resid0, deluxe, panels, coarse_inverse, selector, flags)
    resid1 = resid0 - operator(first, schur)
    second = precondition(resid1, deluxe, panels, coarse_inverse, selector, flags)
    curved = operator(second, schur)
    top = jnp.sum(resid1 * second, axis=(0, 1, 2, 4))
    bottom = jnp.sum(second * curved, axis=(0, 1, 2, 4))
    step_len = top / bottom
    return (first + step_len[:, None] * second).astype(jnp.bfloat16)
```

```python
import jax
import jax.numpy as jnp
from jax import lax
from jax.sharding import PartitionSpec as P


def with_halo(block, sides, width):
    for axis, dim in sides:
        count = lax.axis_size(axis)
        forward = [(i, i + 1) for i in range(count - 1)]
        backward = [(target, source) for source, target in forward]
        low = lax.ppermute(
            lax.slice_in_dim(block, block.shape[dim] - width, None, axis=dim), axis, forward
        )
        high = lax.ppermute(lax.slice_in_dim(block, 0, width, axis=dim), axis, backward)
        block = jnp.concatenate([low, block, high], axis=dim)
    return block


def gather_rows(block, axes):
    count = lax.axis_size(axes)
    spread = jnp.broadcast_to(block[None], (count,) + block.shape)
    swapped = lax.all_to_all(spread, axes, 0, 0, tiled=False)
    return swapped.reshape((count * block.shape[0],) + block.shape[1:])


def sum_over(block, axes):
    return jnp.sum(gather_rows(block[None], axes), axis=0)


def face_mul(vectors, matrices):
    return jnp.einsum("fry,fyx->frx", vectors, matrices, preferred_element_type=jnp.float32)


def face_mul_turned(vectors, matrices):
    return jnp.einsum("fry,fxy->frx", vectors, matrices, preferred_element_type=jnp.float32)


def face_pairs(values):
    along_first = with_halo(values[0:2], (("gx", 0),), 1)
    along_second = with_halo(values[2:4], (("gy", 0),), 1)
    return jnp.stack([along_first[0], along_first[3], along_second[0], along_second[3]], axis=0)


def image_pairs(values):
    along_first = with_halo(values[0:2], (("gx", 0),), 1)
    along_second = with_halo(values[2:4], (("gy", 0),), 1)
    return jnp.stack([along_first[0], along_first[3], along_second[0], along_second[3]], axis=0)


def per_device(load_parts, schur, deluxe, panels, coarse_inverse, primal_dofs, damage_flags):
    loads_here = load_parts[0, 0]
    schur_panel = schur[0, 0]
    deluxe_panel = deluxe[0, 0]
    inverse_panel = panels[0, 0]
    primal_slots = primal_dofs[0, 0]
    flag_values = damage_flags[0, 0]
    width = loads_here.shape[2]
    primal_count = primal_slots.shape[0]
    positions = jnp.arange(4 * width, dtype=jnp.int32)
    picks = (primal_slots[:, None] == positions[None, :]).reshape(primal_count, 4, width)
    picks_half = picks.astype(jnp.bfloat16)
    picks_full = picks.astype(jnp.float32)
    flags_full = flag_values.astype(jnp.float32)

    def add_coarse(piece):
        return jnp.dot(coarse_inverse, piece.astype(jnp.float32), precision=lax.Precision.HIGHEST)

    def precondition(resid):
        scaled = face_mul_turned(resid.astype(jnp.bfloat16), deluxe_panel).astype(jnp.bfloat16)
        local_part = face_mul(scaled, inverse_panel)
        extra = face_mul(local_part.astype(jnp.bfloat16), inverse_panel)
        softened = local_part + 0.5 * flags_full[:, None, None] * extra
        primal = jnp.einsum(
            "kfx,frx->kr", picks_half, scaled, preferred_element_type=jnp.float32
        ).astype(jnp.bfloat16)
        coarse = add_coarse(gather_rows(primal, ("gx", "gy")))
        placed = jnp.einsum("kfx,kr->frx", picks_full, coarse, precision=lax.Precision.HIGHEST)
        weighted = (softened + placed).astype(jnp.bfloat16)
        spread = face_mul(weighted, deluxe_panel).astype(jnp.bfloat16)
        return spread.astype(jnp.float32) + face_pairs(spread).astype(jnp.float32)

    def apply_operator(field):
        bent = face_mul(field.astype(jnp.bfloat16), schur_panel).astype(jnp.bfloat16)
        return bent.astype(jnp.float32) + image_pairs(bent).astype(jnp.float32)

    resid0 = loads_here.astype(jnp.float32) + face_pairs(loads_here).astype(jnp.float32)
    first = precondition(resid0)
    resid1 = resid0 - apply_operator(first)
    second = precondition(resid1)
    curved = apply_operator(second)
    partial = jnp.stack(
        [jnp.sum(resid1 * second, axis=(0, 2)), jnp.sum(second * curved, axis=(0, 2))]
    )
    top, bottom = sum_over(partial, ("gx", "gy"))
    step_len = top / bottom
    result = (first + step_len[:, None] * second).astype(jnp.bfloat16)
    return result[None, None]


def solution(mesh):
    return jax.shard_map(
        per_device,
        mesh=mesh,
        in_specs=(
            P("gx", "gy", None, None, None),
            P("gx", "gy", None, None, None),
            P("gx", "gy", None, None, None),
            P("gx", "gy", None, None, None),
            P(("gx", "gy"), None),
            P("gx", "gy", None),
            P("gx", "gy", None),
        ),
        out_specs=P("gx", "gy", None, None, None),
        check_vma=False,
    )
```

```python
import jax
import jax.numpy as jnp
from jax import lax
from jax.sharding import PartitionSpec as P

PARTNERS = (("gx", True, 1), ("gx", False, 0), ("gy", True, 3), ("gy", False, 2))


def from_partner(values, axis, from_lower):
    count = lax.axis_size(axis)
    if from_lower:
        pairs = [(i, i + 1) for i in range(count - 1)]
    else:
        pairs = [(i + 1, i) for i in range(count - 1)]
    return lax.ppermute(values, axis, pairs)


def gather_rows(block, axes):
    count = lax.axis_size(axes)
    spread = jnp.broadcast_to(block[None], (count,) + block.shape)
    swapped = lax.all_to_all(spread, axes, 0, 0, tiled=False)
    return swapped.reshape((count * block.shape[0],) + block.shape[1:])


def sum_over(block, axes):
    return jnp.sum(gather_rows(block[None], axes), axis=0)


def face_mul(vectors, matrices):
    return jnp.einsum("fry,fyx->frx", vectors, matrices, preferred_element_type=jnp.float32)


def to_half(values):
    return lax.reduce_precision(values, exponent_bits=8, mantissa_bits=7)


def face_mul_turned(vectors, matrices):
    return jnp.einsum("fry,fxy->frx", vectors, matrices, preferred_element_type=jnp.float32)


def per_device(load_parts, schur, deluxe, panels, coarse_inverse, primal_dofs, damage_flags):
    loads_here = load_parts[0, 0]
    schur_own = schur[0, 0]
    deluxe_own = deluxe[0, 0]
    panels_own = panels[0, 0]
    primal_slots = primal_dofs[0, 0]
    flag_values = damage_flags[0, 0]
    width = loads_here.shape[2]
    primal_count = primal_slots.shape[0]
    rows = coarse_inverse.shape[1]

    small = jnp.concatenate(
        [
            coarse_inverse,
            jnp.pad(
                jnp.concatenate([primal_slots, flag_values]).astype(jnp.float32)[None],
                ((0, 0), (0, rows - 2 * primal_count)),
            ),
        ]
    )
    load_partner, mats_partner, small_partner = [], [], []
    for axis, from_lower, face in PARTNERS:
        load_partner.append(from_partner(loads_here[face], axis, from_lower))
        small_partner.append(from_partner(small, axis, from_lower))
        mats = jnp.stack([deluxe_own[face], panels_own[face], schur_own[face]])
        mats_partner.append(from_partner(mats, axis, from_lower))
    load_partner = jnp.stack(load_partner)
    mats_partner = jnp.stack(mats_partner)
    small_partner = jnp.stack(small_partner)
    deluxe_partner = mats_partner[:, 0]
    panels_partner = mats_partner[:, 1]
    schur_partner = mats_partner[:, 2]

    coarse_rows = jnp.concatenate(
        [coarse_inverse, small_partner[:, :primal_count].reshape(-1, small_partner.shape[2])]
    )
    partner_slots = small_partner[:, primal_count, :primal_count].astype(jnp.int32)
    partner_flags = jnp.stack(
        [small_partner[p, primal_count, primal_count + face] for p, (_, _, face) in enumerate(PARTNERS)]
    )
    partner_offsets = jnp.array([face * width for _, _, face in PARTNERS], jnp.int32)

    positions = jnp.arange(4 * width, dtype=jnp.int32)
    picks = (primal_slots[:, None] == positions[None, :]).reshape(primal_count, 4, width)
    picks_half = picks.astype(jnp.bfloat16)
    picks_full = picks.astype(jnp.float32)
    flags_full = flag_values.astype(jnp.float32)
    face_positions = jnp.arange(width, dtype=jnp.int32)
    partner_picks = (
        partner_slots[:, :, None] == (partner_offsets[:, None, None] + face_positions[None, None, :])
    ).astype(jnp.float32)

    def local_side(resid_half, deluxe_panel, inverse_panel, flags):
        scaled = face_mul_turned(resid_half, deluxe_panel).astype(jnp.bfloat16)
        local_part = face_mul(scaled, inverse_panel)
        extra = face_mul(local_part.astype(jnp.bfloat16), inverse_panel)
        return scaled, local_part + 0.5 * flags[:, None, None] * extra

    def precondition(resid):
        resid_half = resid.astype(jnp.bfloat16)
        scaled, softened_own = local_side(resid_half, deluxe_own, panels_own, flags_full)
        _, softened_partner = local_side(resid_half, deluxe_partner, panels_partner, partner_flags)
        primal = jnp.einsum(
            "kfx,frx->kr", picks_half, scaled, preferred_element_type=jnp.float32
        ).astype(jnp.bfloat16)
        primal_all = gather_rows(primal, ("gx", "gy")).astype(jnp.float32)
        coarse = jnp.dot(coarse_rows, primal_all, precision=lax.Precision.HIGHEST)
        coarse_own = coarse[:primal_count]
        coarse_partner = coarse[primal_count:].reshape(4, primal_count, -1)
        placed_own = jnp.einsum("kfx,kr->frx", picks_full, coarse_own, precision=lax.Precision.HIGHEST)
        placed_partner = jnp.einsum(
            "pkx,pkr->prx", partner_picks, coarse_partner, precision=lax.Precision.HIGHEST
        )
        weighted_own = (softened_own + placed_own).astype(jnp.bfloat16)
        weighted_partner = (softened_partner + placed_partner).astype(jnp.bfloat16)
        spread_own = to_half(face_mul(weighted_own, deluxe_own))
        spread_partner = to_half(face_mul(weighted_partner, deluxe_partner))
        return spread_own + spread_partner

    def apply_operator(field):
        field_half = field.astype(jnp.bfloat16)
        bent_own = to_half(face_mul(field_half, schur_own))
        bent_partner = to_half(face_mul(field_half, schur_partner))
        return bent_own + bent_partner

    resid0 = loads_here.astype(jnp.float32) + load_partner.astype(jnp.float32)
    first = precondition(resid0)
    resid1 = resid0 - apply_operator(first)
    second = precondition(resid1)
    curved = apply_operator(second)
    partial = jnp.stack(
        [jnp.sum(resid1 * second, axis=(0, 2)), jnp.sum(second * curved, axis=(0, 2))]
    )
    top, bottom = sum_over(partial, ("gx", "gy"))
    step_len = top / bottom
    result = (first + step_len[:, None] * second).astype(jnp.bfloat16)
    return result[None, None]


def solution(mesh):
    return jax.shard_map(
        per_device,
        mesh=mesh,
        in_specs=(
            P("gx", "gy", None, None, None),
            P("gx", "gy", None, None, None),
            P("gx", "gy", None, None, None),
            P("gx", "gy", None, None, None),
            P(("gx", "gy"), None),
            P("gx", "gy", None),
            P("gx", "gy", None),
        ),
        out_specs=P("gx", "gy", None, None, None),
        check_vma=False,
    )
```

```python
import jax
import jax.numpy as jnp
from jax import lax
from jax.sharding import PartitionSpec as P


def with_halo(block, sides, width):
    for axis, dim in sides:
        count = lax.axis_size(axis)
        forward = [(i, i + 1) for i in range(count - 1)]
        backward = [(target, source) for source, target in forward]
        low = lax.ppermute(
            lax.slice_in_dim(block, block.shape[dim] - width, None, axis=dim), axis, forward
        )
        high = lax.ppermute(lax.slice_in_dim(block, 0, width, axis=dim), axis, backward)
        block = jnp.concatenate([low, block, high], axis=dim)
    return block


def gather_rows(block, axes):
    count = lax.axis_size(axes)
    spread = jnp.broadcast_to(block[None], (count,) + block.shape)
    swapped = lax.all_to_all(spread, axes, 0, 0, tiled=False)
    return swapped.reshape((count * block.shape[0],) + block.shape[1:])


def sum_over(block, axes):
    return jnp.sum(gather_rows(block[None], axes), axis=0)


PARTNERS = (("gx", True, 1), ("gx", False, 0), ("gy", True, 3), ("gy", False, 2))


def from_partner(values, axis, from_lower):
    count = lax.axis_size(axis)
    if from_lower:
        pairs = [(i, i + 1) for i in range(count - 1)]
    else:
        pairs = [(i + 1, i) for i in range(count - 1)]
    return lax.ppermute(values, axis, pairs)


def to_half(values):
    return lax.reduce_precision(values, exponent_bits=8, mantissa_bits=7)


def face_mul(vectors, matrices):
    return jnp.einsum("fry,fyx->frx", vectors, matrices, preferred_element_type=jnp.float32)


def face_mul_turned(vectors, matrices):
    return jnp.einsum("fry,fxy->frx", vectors, matrices, preferred_element_type=jnp.float32)


def face_pairs(values):
    along_first = with_halo(values[0:2], (("gx", 0),), 1)
    along_second = with_halo(values[2:4], (("gy", 0),), 1)
    return jnp.stack([along_first[0], along_first[3], along_second[0], along_second[3]], axis=0)


def per_device(load_parts, schur, deluxe, panels, coarse_inverse, primal_dofs, damage_flags):
    loads_here = load_parts[0, 0]
    schur_panel = schur[0, 0]
    deluxe_panel = deluxe[0, 0]
    inverse_panel = panels[0, 0]
    primal_slots = primal_dofs[0, 0]
    flag_values = damage_flags[0, 0]
    width = loads_here.shape[2]
    primal_count = primal_slots.shape[0]
    positions = jnp.arange(4 * width, dtype=jnp.int32)
    picks = (primal_slots[:, None] == positions[None, :]).reshape(primal_count, 4, width)
    picks_half = picks.astype(jnp.bfloat16)
    picks_full = picks.astype(jnp.float32)
    flags_full = flag_values.astype(jnp.float32)

    def add_coarse(piece):
        return jnp.dot(coarse_inverse, piece.astype(jnp.float32), precision=lax.Precision.HIGHEST)

    def precondition(resid):
        scaled = face_mul_turned(resid.astype(jnp.bfloat16), deluxe_panel).astype(jnp.bfloat16)
        local_part = face_mul(scaled, inverse_panel)
        extra = face_mul(local_part.astype(jnp.bfloat16), inverse_panel)
        softened = local_part + 0.5 * flags_full[:, None, None] * extra
        primal = jnp.einsum(
            "kfx,frx->kr", picks_half, scaled, preferred_element_type=jnp.float32
        ).astype(jnp.bfloat16)
        coarse = add_coarse(gather_rows(primal, ("gx", "gy")))
        placed = jnp.einsum("kfx,kr->frx", picks_full, coarse, precision=lax.Precision.HIGHEST)
        weighted = (softened + placed).astype(jnp.bfloat16)
        spread = face_mul(weighted, deluxe_panel).astype(jnp.bfloat16)
        return spread.astype(jnp.float32) + face_pairs(spread).astype(jnp.float32)

    schur_partner = jnp.stack(
        [from_partner(schur_panel[face], axis, from_lower) for axis, from_lower, face in PARTNERS]
    )

    def apply_operator(field):
        field_half = field.astype(jnp.bfloat16)
        bent_own = to_half(face_mul(field_half, schur_panel))
        bent_partner = to_half(face_mul(field_half, schur_partner))
        return bent_own + bent_partner

    resid0 = loads_here.astype(jnp.float32) + face_pairs(loads_here).astype(jnp.float32)
    first = precondition(resid0)
    resid1 = resid0 - apply_operator(first)
    second = precondition(resid1)
    curved = apply_operator(second)
    partial = jnp.stack(
        [jnp.sum(resid1 * second, axis=(0, 2)), jnp.sum(second * curved, axis=(0, 2))]
    )
    top, bottom = sum_over(partial, ("gx", "gy"))
    step_len = top / bottom
    result = (first + step_len[:, None] * second).astype(jnp.bfloat16)
    return result[None, None]


def solution(mesh):
    return jax.shard_map(
        per_device,
        mesh=mesh,
        in_specs=(
            P("gx", "gy", None, None, None),
            P("gx", "gy", None, None, None),
            P("gx", "gy", None, None, None),
            P("gx", "gy", None, None, None),
            P(("gx", "gy"), None),
            P("gx", "gy", None),
            P("gx", "gy", None),
        ),
        out_specs=P("gx", "gy", None, None, None),
        check_vma=False,
    )
```

```python
import jax
import jax.numpy as jnp
from jax import lax
from jax.sharding import PartitionSpec as P


def with_halo(block, sides, width):
    for axis, dim in sides:
        count = lax.axis_size(axis)
        forward = [(i, i + 1) for i in range(count - 1)]
        backward = [(target, source) for source, target in forward]
        low = lax.ppermute(
            lax.slice_in_dim(block, block.shape[dim] - width, None, axis=dim), axis, forward
        )
        high = lax.ppermute(lax.slice_in_dim(block, 0, width, axis=dim), axis, backward)
        block = jnp.concatenate([low, block, high], axis=dim)
    return block


def gather_rows(block, axes):
    count = lax.axis_size(axes)
    spread = jnp.broadcast_to(block[None], (count,) + block.shape)
    swapped = lax.all_to_all(spread, axes, 0, 0, tiled=False)
    return swapped.reshape((count * block.shape[0],) + block.shape[1:])


def sum_over(block, axes):
    return jnp.sum(gather_rows(block[None], axes), axis=0)


PARTNERS = (("gx", True, 1), ("gx", False, 0), ("gy", True, 3), ("gy", False, 2))


def from_partner(values, axis, from_lower):
    count = lax.axis_size(axis)
    if from_lower:
        pairs = [(i, i + 1) for i in range(count - 1)]
    else:
        pairs = [(i + 1, i) for i in range(count - 1)]
    return lax.ppermute(values, axis, pairs)


def to_half(values):
    return lax.reduce_precision(values, exponent_bits=8, mantissa_bits=7)


def face_mul(vectors, matrices):
    return jnp.einsum("fry,fyx->frx", vectors, matrices, preferred_element_type=jnp.float32)


def face_mul_turned(vectors, matrices):
    return jnp.einsum("fry,fxy->frx", vectors, matrices, preferred_element_type=jnp.float32)


def face_pairs(values):
    along_first = with_halo(values[0:2], (("gx", 0),), 1)
    along_second = with_halo(values[2:4], (("gy", 0),), 1)
    return jnp.stack([along_first[0], along_first[3], along_second[0], along_second[3]], axis=0)


def per_device(load_parts, schur, deluxe, panels, coarse_inverse, primal_dofs, damage_flags):
    loads_here = load_parts[0, 0]
    schur_panel = schur[0, 0]
    deluxe_panel = deluxe[0, 0]
    inverse_panel = panels[0, 0]
    primal_slots = primal_dofs[0, 0]
    flag_values = damage_flags[0, 0]
    width = loads_here.shape[2]
    primal_count = primal_slots.shape[0]
    positions = jnp.arange(4 * width, dtype=jnp.int32)
    picks = (primal_slots[:, None] == positions[None, :]).reshape(primal_count, 4, width)
    picks_half = picks.astype(jnp.bfloat16)
    picks_full = picks.astype(jnp.float32)
    flags_full = flag_values.astype(jnp.float32)

    def add_coarse(rows, piece):
        return jnp.dot(rows, piece, precision=lax.Precision.HIGHEST)

    partner_mats = jnp.stack(
        [
            from_partner(jnp.stack([deluxe_panel[face], schur_panel[face]]), axis, from_lower)
            for axis, from_lower, face in PARTNERS
        ]
    )
    deluxe_partner = partner_mats[:, 0]
    schur_partner = partner_mats[:, 1]

    own_small = jnp.concatenate(
        [coarse_inverse.reshape(-1), primal_slots.astype(jnp.float32)]
    )
    small_rows = -(-own_small.shape[0] // width)
    own_small = jnp.pad(own_small, (0, small_rows * width - own_small.shape[0])).reshape(
        small_rows, width
    )
    face_positions = jnp.arange(width, dtype=jnp.int32)
    partner_offsets = jnp.array([face * width for _, _, face in PARTNERS], jnp.int32)

    def precondition(resid, partner_small):
        scaled = face_mul_turned(resid.astype(jnp.bfloat16), deluxe_panel).astype(jnp.bfloat16)
        local_part = face_mul(scaled, inverse_panel)
        extra = face_mul(local_part.astype(jnp.bfloat16), inverse_panel)
        softened = local_part + 0.5 * flags_full[:, None, None] * extra
        received = []
        for axis, from_lower, face in PARTNERS:
            payload = softened[face]
            if partner_small is None:
                payload = jnp.concatenate([payload, own_small])
            received.append(from_partner(payload, axis, from_lower))
        received = jnp.stack(received)
        softened_partner = received[:, : resid.shape[1]]
        if partner_small is None:
            partner_small = received[:, resid.shape[1] :].reshape(4, -1)
        partner_rows = partner_small[:, : coarse_inverse.size].reshape(-1, coarse_inverse.shape[1])
        partner_slots = partner_small[:, coarse_inverse.size : coarse_inverse.size + primal_count]
        partner_picks = (
            partner_slots.astype(jnp.int32)[:, :, None]
            == (partner_offsets[:, None, None] + face_positions[None, None, :])
        ).astype(jnp.float32)

        primal = jnp.einsum(
            "kfx,frx->kr", picks_half, scaled, preferred_element_type=jnp.float32
        ).astype(jnp.bfloat16)
        primal_all = gather_rows(primal, ("gx", "gy")).astype(jnp.float32)
        coarse = add_coarse(coarse_inverse, primal_all)
        coarse_partner = add_coarse(partner_rows, primal_all).reshape(4, primal_count, -1)
        placed = jnp.einsum("kfx,kr->frx", picks_full, coarse, precision=lax.Precision.HIGHEST)
        placed_partner = jnp.sum(partner_picks[:, :, None, :] * coarse_partner[:, :, :, None], axis=1)
        weighted = (softened + placed).astype(jnp.bfloat16)
        weighted_partner = (softened_partner + placed_partner).astype(jnp.bfloat16)
        spread = to_half(face_mul(weighted, deluxe_panel))
        spread_partner = to_half(face_mul(weighted_partner, deluxe_partner))
        return spread + spread_partner, partner_small

    def apply_operator(field):
        field_half = field.astype(jnp.bfloat16)
        bent_own = to_half(face_mul(field_half, schur_panel))
        bent_partner = to_half(face_mul(field_half, schur_partner))
        return bent_own + bent_partner

    resid0 = loads_here.astype(jnp.float32) + face_pairs(loads_here).astype(jnp.float32)
    first, partner_small = precondition(resid0, None)
    resid1 = resid0 - apply_operator(first)
    second, _ = precondition(resid1, partner_small)
    curved = apply_operator(second)
    partial = jnp.stack(
        [jnp.sum(resid1 * second, axis=(0, 2)), jnp.sum(second * curved, axis=(0, 2))]
    )
    top, bottom = sum_over(partial, ("gx", "gy"))
    step_len = top / bottom
    result = (first + step_len[:, None] * second).astype(jnp.bfloat16)
    return result[None, None]


def solution(mesh):
    return jax.shard_map(
        per_device,
        mesh=mesh,
        in_specs=(
            P("gx", "gy", None, None, None),
            P("gx", "gy", None, None, None),
            P("gx", "gy", None, None, None),
            P("gx", "gy", None, None, None),
            P(("gx", "gy"), None),
            P("gx", "gy", None),
            P("gx", "gy", None),
        ),
        out_specs=P("gx", "gy", None, None, None),
        check_vma=False,
    )
```

```python
import jax
import jax.numpy as jnp
from jax import lax
from jax.sharding import PartitionSpec as P


def with_halo(block, sides, width):
    for axis, dim in sides:
        count = lax.axis_size(axis)
        forward = [(i, i + 1) for i in range(count - 1)]
        backward = [(target, source) for source, target in forward]
        low = lax.ppermute(
            lax.slice_in_dim(block, block.shape[dim] - width, None, axis=dim), axis, forward
        )
        high = lax.ppermute(lax.slice_in_dim(block, 0, width, axis=dim), axis, backward)
        block = jnp.concatenate([low, block, high], axis=dim)
    return block


def gather_rows(block, axes):
    count = lax.axis_size(axes)
    spread = jnp.broadcast_to(block[None], (count,) + block.shape)
    swapped = lax.all_to_all(spread, axes, 0, 0, tiled=False)
    return swapped.reshape((count * block.shape[0],) + block.shape[1:])


def sum_over(block, axes):
    return jnp.sum(gather_rows(block[None], axes), axis=0)


PARTNERS = (("gx", True, 1), ("gx", False, 0), ("gy", True, 3), ("gy", False, 2))


def from_partner(values, axis, from_lower):
    count = lax.axis_size(axis)
    if from_lower:
        pairs = [(i, i + 1) for i in range(count - 1)]
    else:
        pairs = [(i + 1, i) for i in range(count - 1)]
    return lax.ppermute(values, axis, pairs)


def to_half(values):
    return lax.reduce_precision(values, exponent_bits=8, mantissa_bits=7)


def face_mul(vectors, matrices):
    return jnp.einsum("fry,fyx->frx", vectors, matrices, preferred_element_type=jnp.float32)


def face_mul_turned(vectors, matrices):
    return jnp.einsum("fry,fxy->frx", vectors, matrices, preferred_element_type=jnp.float32)


def face_pairs(values):
    along_first = with_halo(values[0:2], (("gx", 0),), 1)
    along_second = with_halo(values[2:4], (("gy", 0),), 1)
    return jnp.stack([along_first[0], along_first[3], along_second[0], along_second[3]], axis=0)


def per_device(load_parts, schur, deluxe, panels, coarse_inverse, primal_dofs, damage_flags):
    loads_here = load_parts[0, 0]
    schur_panel = schur[0, 0]
    deluxe_panel = deluxe[0, 0]
    inverse_panel = panels[0, 0]
    primal_slots = primal_dofs[0, 0]
    flag_values = damage_flags[0, 0]
    width = loads_here.shape[2]
    primal_count = primal_slots.shape[0]
    positions = jnp.arange(4 * width, dtype=jnp.int32)
    picks = (primal_slots[:, None] == positions[None, :]).reshape(primal_count, 4, width)
    picks_half = picks.astype(jnp.bfloat16)
    picks_full = picks.astype(jnp.float32)
    flags_full = flag_values.astype(jnp.float32)

    def add_coarse(piece):
        return jnp.dot(coarse_inverse, piece.astype(jnp.float32), precision=lax.Precision.HIGHEST)

    def precondition(resid, schur_partner):
        scaled = face_mul_turned(resid.astype(jnp.bfloat16), deluxe_panel).astype(jnp.bfloat16)
        local_part = face_mul(scaled, inverse_panel)
        extra = face_mul(local_part.astype(jnp.bfloat16), inverse_panel)
        softened = local_part + 0.5 * flags_full[:, None, None] * extra
        primal = jnp.einsum(
            "kfx,frx->kr", picks_half, scaled, preferred_element_type=jnp.float32
        ).astype(jnp.bfloat16)
        coarse = add_coarse(gather_rows(primal, ("gx", "gy")))
        placed = jnp.einsum("kfx,kr->frx", picks_full, coarse, precision=lax.Precision.HIGHEST)
        weighted = (softened + placed).astype(jnp.bfloat16)
        spread = face_mul(weighted, deluxe_panel).astype(jnp.bfloat16)
        if schur_partner is not None:
            return spread.astype(jnp.float32) + face_pairs(spread).astype(jnp.float32), schur_partner
        received = jnp.stack(
            [
                from_partner(jnp.concatenate([spread[face], schur_panel[face]]), axis, from_lower)
                for axis, from_lower, face in PARTNERS
            ]
        )
        rows = spread.shape[1]
        spread_partner = received[:, :rows]
        return spread.astype(jnp.float32) + spread_partner.astype(jnp.float32), received[:, rows:]

    def apply_operator(field, schur_partner):
        field_half = field.astype(jnp.bfloat16)
        bent_own = to_half(face_mul(field_half, schur_panel))
        bent_partner = to_half(face_mul(field_half, schur_partner))
        return bent_own + bent_partner

    resid0 = loads_here.astype(jnp.float32) + face_pairs(loads_here).astype(jnp.float32)
    first, schur_partner = precondition(resid0, None)
    resid1 = resid0 - apply_operator(first, schur_partner)
    second, _ = precondition(resid1, schur_partner)
    curved = apply_operator(second, schur_partner)
    partial = jnp.stack(
        [jnp.sum(resid1 * second, axis=(0, 2)), jnp.sum(second * curved, axis=(0, 2))]
    )
    top, bottom = sum_over(partial, ("gx", "gy"))
    step_len = top / bottom
    result = (first + step_len[:, None] * second).astype(jnp.bfloat16)
    return result[None, None]


def solution(mesh):
    return jax.shard_map(
        per_device,
        mesh=mesh,
        in_specs=(
            P("gx", "gy", None, None, None),
            P("gx", "gy", None, None, None),
            P("gx", "gy", None, None, None),
            P("gx", "gy", None, None, None),
            P(("gx", "gy"), None),
            P("gx", "gy", None),
            P("gx", "gy", None),
        ),
        out_specs=P("gx", "gy", None, None, None),
        check_vma=False,
    )
```

```python
import jax
import jax.numpy as jnp
from jax import lax
from jax.sharding import PartitionSpec as P


def with_halo(block, sides, width):
    for axis, dim in sides:
        count = lax.axis_size(axis)
        forward = [(i, i + 1) for i in range(count - 1)]
        backward = [(target, source) for source, target in forward]
        low = lax.ppermute(
            lax.slice_in_dim(block, block.shape[dim] - width, None, axis=dim), axis, forward
        )
        high = lax.ppermute(lax.slice_in_dim(block, 0, width, axis=dim), axis, backward)
        block = jnp.concatenate([low, block, high], axis=dim)
    return block


def gather_blocks(block, axes):
    count = lax.axis_size(axes)
    spread = jnp.broadcast_to(block[None], (count,) + block.shape)
    return lax.all_to_all(spread, axes, 0, 0, tiled=False)


def gather_rows(block, axes):
    count = lax.axis_size(axes)
    spread = jnp.broadcast_to(block[None], (count,) + block.shape)
    swapped = lax.all_to_all(spread, axes, 0, 0, tiled=False)
    return swapped.reshape((count * block.shape[0],) + block.shape[1:])


def sum_over(block, axes):
    return jnp.sum(gather_rows(block[None], axes), axis=0)


PARTNERS = (("gx", True, 1), ("gx", False, 0), ("gy", True, 3), ("gy", False, 2))


def from_partner(values, axis, from_lower):
    count = lax.axis_size(axis)
    if from_lower:
        pairs = [(i, i + 1) for i in range(count - 1)]
    else:
        pairs = [(i + 1, i) for i in range(count - 1)]
    return lax.ppermute(values, axis, pairs)


def to_half(values):
    return lax.reduce_precision(values, exponent_bits=8, mantissa_bits=7)


def face_mul(vectors, matrices):
    return jnp.einsum("fry,fyx->frx", vectors, matrices, preferred_element_type=jnp.float32)


def face_mul_turned(vectors, matrices):
    return jnp.einsum("fry,fxy->frx", vectors, matrices, preferred_element_type=jnp.float32)


def face_pairs(values):
    along_first = with_halo(values[0:2], (("gx", 0),), 1)
    along_second = with_halo(values[2:4], (("gy", 0),), 1)
    return jnp.stack([along_first[0], along_first[3], along_second[0], along_second[3]], axis=0)


def per_device(load_parts, schur, deluxe, panels, coarse_inverse, primal_dofs, damage_flags):
    loads_here = load_parts[0, 0]
    schur_panel = schur[0, 0]
    deluxe_panel = deluxe[0, 0]
    inverse_panel = panels[0, 0]
    primal_slots = primal_dofs[0, 0]
    flag_values = damage_flags[0, 0]
    width = loads_here.shape[2]
    primal_count = primal_slots.shape[0]
    positions = jnp.arange(4 * width, dtype=jnp.int32)
    picks = (primal_slots[:, None] == positions[None, :]).reshape(primal_count, 4, width)
    picks_half = picks.astype(jnp.bfloat16)
    picks_full = picks.astype(jnp.float32)
    flags_full = flag_values.astype(jnp.float32)

    def precondition(resid, schur_partner):
        scaled = face_mul_turned(resid.astype(jnp.bfloat16), deluxe_panel).astype(jnp.bfloat16)
        local_part = face_mul(scaled, inverse_panel)
        extra = face_mul(local_part.astype(jnp.bfloat16), inverse_panel)
        softened = local_part + 0.5 * flags_full[:, None, None] * extra
        primal = jnp.einsum(
            "kfx,frx->kr", picks_half, scaled, preferred_element_type=jnp.float32
        ).astype(jnp.bfloat16)
        gathered = gather_blocks(primal, ("gx", "gy")).astype(jnp.float32)
        coarse = jnp.einsum(
            "ijk,jkr->ir",
            coarse_inverse.reshape(primal_count, gathered.shape[0], gathered.shape[1]),
            gathered,
            precision=lax.Precision.HIGHEST,
        )
        placed = jnp.sum(picks_full[:, :, None, :] * coarse[:, None, :, None], axis=0)
        weighted = (softened + placed).astype(jnp.bfloat16)
        spread = face_mul(weighted, deluxe_panel).astype(jnp.bfloat16)
        if schur_partner is not None:
            return spread.astype(jnp.float32) + face_pairs(spread).astype(jnp.float32), schur_partner
        received = jnp.stack(
            [
                from_partner(jnp.concatenate([spread[face], schur_panel[face]]), axis, from_lower)
                for axis, from_lower, face in PARTNERS
            ]
        )
        rows = spread.shape[1]
        spread_partner = received[:, :rows]
        return spread.astype(jnp.float32) + spread_partner.astype(jnp.float32), received[:, rows:]

    def apply_operator(field, schur_partner):
        field_half = field.astype(jnp.bfloat16)
        bent_own = to_half(face_mul(field_half, schur_panel))
        bent_partner = to_half(face_mul(field_half, schur_partner))
        return bent_own + bent_partner

    resid0 = loads_here.astype(jnp.float32) + face_pairs(loads_here).astype(jnp.float32)
    first, schur_partner = precondition(resid0, None)
    resid1 = resid0 - apply_operator(first, schur_partner)
    second, _ = precondition(resid1, schur_partner)
    curved = apply_operator(second, schur_partner)
    partial = jnp.stack(
        [jnp.sum(resid1 * second, axis=(0, 2)), jnp.sum(second * curved, axis=(0, 2))]
    )
    top, bottom = sum_over(partial, ("gx", "gy"))
    step_len = top / bottom
    result = (first + step_len[:, None] * second).astype(jnp.bfloat16)
    return result[None, None]


def solution(mesh):
    return jax.shard_map(
        per_device,
        mesh=mesh,
        in_specs=(
            P("gx", "gy", None, None, None),
            P("gx", "gy", None, None, None),
            P("gx", "gy", None, None, None),
            P("gx", "gy", None, None, None),
            P(("gx", "gy"), None),
            P("gx", "gy", None),
            P("gx", "gy", None),
        ),
        out_specs=P("gx", "gy", None, None, None),
        check_vma=False,
    )
```

```python
import jax
import jax.numpy as jnp
from jax import lax
from jax.sharding import PartitionSpec as P


def with_halo(block, sides, width):
    for axis, dim in sides:
        count = lax.axis_size(axis)
        forward = [(i, i + 1) for i in range(count - 1)]
        backward = [(target, source) for source, target in forward]
        low = lax.ppermute(
            lax.slice_in_dim(block, block.shape[dim] - width, None, axis=dim), axis, forward
        )
        high = lax.ppermute(lax.slice_in_dim(block, 0, width, axis=dim), axis, backward)
        block = jnp.concatenate([low, block, high], axis=dim)
    return block


def gather_rows(block, axes):
    count = lax.axis_size(axes)
    spread = jnp.broadcast_to(block[None], (count,) + block.shape)
    swapped = lax.all_to_all(spread, axes, 0, 0, tiled=False)
    return swapped.reshape((count * block.shape[0],) + block.shape[1:])


def sum_over(block, axes):
    return jnp.sum(gather_rows(block[None], axes), axis=0)


PARTNERS = (("gx", True, 1), ("gx", False, 0), ("gy", True, 3), ("gy", False, 2))


def from_partner(values, axis, from_lower):
    count = lax.axis_size(axis)
    if from_lower:
        pairs = [(i, i + 1) for i in range(count - 1)]
    else:
        pairs = [(i + 1, i) for i in range(count - 1)]
    return lax.ppermute(values, axis, pairs)


def to_half(values):
    return lax.reduce_precision(values, exponent_bits=8, mantissa_bits=7)


def face_mul(vectors, matrices):
    return jnp.einsum("fry,fyx->frx", vectors, matrices, preferred_element_type=jnp.float32)


def face_mul_turned(vectors, matrices):
    return jnp.einsum("fry,fxy->frx", vectors, matrices, preferred_element_type=jnp.float32)


def face_pairs(values):
    along_first = with_halo(values[0:2], (("gx", 0),), 1)
    along_second = with_halo(values[2:4], (("gy", 0),), 1)
    return jnp.stack([along_first[0], along_first[3], along_second[0], along_second[3]], axis=0)


def per_device(load_parts, schur, deluxe, panels, coarse_inverse, primal_dofs, damage_flags):
    loads_here = load_parts[0, 0]
    schur_panel = schur[0, 0]
    deluxe_panel = deluxe[0, 0]
    inverse_panel = panels[0, 0]
    primal_slots = primal_dofs[0, 0]
    flag_values = damage_flags[0, 0]
    width = loads_here.shape[2]
    primal_count = primal_slots.shape[0]
    positions = jnp.arange(4 * width, dtype=jnp.int32)
    picks = (primal_slots[:, None] == positions[None, :]).reshape(primal_count, 4, width)
    picks_half = picks.astype(jnp.bfloat16)
    picks_full = picks.astype(jnp.float32)
    flags_full = flag_values.astype(jnp.float32)

    def add_coarse(piece):
        return jnp.dot(coarse_inverse, piece.astype(jnp.float32), precision=lax.Precision.HIGHEST)

    def precondition(resid, carried):
        scaled = face_mul_turned(resid.astype(jnp.bfloat16), deluxe_panel).astype(jnp.bfloat16)
        local_part = face_mul(scaled, inverse_panel)
        extra = face_mul(local_part.astype(jnp.bfloat16), inverse_panel)
        softened = local_part + 0.5 * flags_full[:, None, None] * extra
        primal = jnp.einsum(
            "kfx,frx->kr", picks_half, scaled, preferred_element_type=jnp.float32
        ).astype(jnp.bfloat16)
        if carried is not None:
            carried, primal = lax.optimization_barrier((carried, primal))
        coarse = add_coarse(gather_rows(primal, ("gx", "gy")))
        placed = jnp.einsum("kfx,kr->frx", picks_full, coarse, precision=lax.Precision.HIGHEST)
        weighted = (softened + placed).astype(jnp.bfloat16)
        spread = face_mul(weighted, deluxe_panel).astype(jnp.bfloat16)
        return spread.astype(jnp.float32) + face_pairs(spread).astype(jnp.float32), carried

    def apply_operator(field):
        field_half = field.astype(jnp.bfloat16)
        bent_own = to_half(face_mul(field_half, schur_panel))
        bent_partner = to_half(face_mul(field_half, schur_partner))
        return bent_own + bent_partner

    rows = loads_here.shape[1]
    halo = []
    for axis, from_lower, face in PARTNERS:
        payload = loads_here[face]
        if axis == "gy":
            payload = jnp.concatenate([payload, schur_panel[face]])
        halo.append(from_partner(payload, axis, from_lower))
    load_partner = jnp.stack([received[:rows] for received in halo])
    resid0 = loads_here.astype(jnp.float32) + load_partner.astype(jnp.float32)
    first, schur_along_x = precondition(resid0, schur_panel[0:2])
    schur_partner = jnp.stack(
        [from_partner(schur_along_x[face], axis, from_lower) for axis, from_lower, face in PARTNERS[:2]]
        + [received[rows:] for received in halo[2:]]
    )
    resid1 = resid0 - apply_operator(first)
    second, _ = precondition(resid1, None)
    curved = apply_operator(second)
    partial = jnp.stack(
        [jnp.sum(resid1 * second, axis=(0, 2)), jnp.sum(second * curved, axis=(0, 2))]
    )
    top, bottom = sum_over(partial, ("gx", "gy"))
    step_len = top / bottom
    result = (first + step_len[:, None] * second).astype(jnp.bfloat16)
    return result[None, None]


def solution(mesh):
    return jax.shard_map(
        per_device,
        mesh=mesh,
        in_specs=(
            P("gx", "gy", None, None, None),
            P("gx", "gy", None, None, None),
            P("gx", "gy", None, None, None),
            P("gx", "gy", None, None, None),
            P(("gx", "gy"), None),
            P("gx", "gy", None),
            P("gx", "gy", None),
        ),
        out_specs=P("gx", "gy", None, None, None),
        check_vma=False,
    )
```

```python
import jax
import jax.numpy as jnp
from jax import lax
from jax.sharding import PartitionSpec as P


def with_halo(block, sides, width):
    for axis, dim in sides:
        count = lax.axis_size(axis)
        forward = [(i, i + 1) for i in range(count - 1)]
        backward = [(target, source) for source, target in forward]
        low = lax.ppermute(
            lax.slice_in_dim(block, block.shape[dim] - width, None, axis=dim), axis, forward
        )
        high = lax.ppermute(lax.slice_in_dim(block, 0, width, axis=dim), axis, backward)
        block = jnp.concatenate([low, block, high], axis=dim)
    return block


def gather_rows(block, axes):
    count = lax.axis_size(axes)
    spread = jnp.broadcast_to(block[None], (count,) + block.shape)
    swapped = lax.all_to_all(spread, axes, 0, 0, tiled=False)
    return swapped.reshape((count * block.shape[0],) + block.shape[1:])


def sum_over(block, axes):
    return jnp.sum(gather_rows(block[None], axes), axis=0)


PARTNERS = (("gx", True, 1), ("gx", False, 0), ("gy", True, 3), ("gy", False, 2))


def from_partner(values, axis, from_lower):
    count = lax.axis_size(axis)
    if from_lower:
        pairs = [(i, i + 1) for i in range(count - 1)]
    else:
        pairs = [(i + 1, i) for i in range(count - 1)]
    return lax.ppermute(values, axis, pairs)


def to_half(values):
    return lax.reduce_precision(values, exponent_bits=8, mantissa_bits=7)


def face_mul(vectors, matrices):
    return jnp.einsum("fry,fyx->frx", vectors, matrices, preferred_element_type=jnp.float32)


def face_mul_turned(vectors, matrices):
    return jnp.einsum("fry,fxy->frx", vectors, matrices, preferred_element_type=jnp.float32)


def face_pairs(values):
    along_first = with_halo(values[0:2], (("gx", 0),), 1)
    along_second = with_halo(values[2:4], (("gy", 0),), 1)
    return jnp.stack([along_first[0], along_first[3], along_second[0], along_second[3]], axis=0)


def per_device(load_parts, schur, deluxe, panels, coarse_inverse, primal_dofs, damage_flags):
    loads_here = load_parts[0, 0]
    schur_panel = schur[0, 0]
    deluxe_panel = deluxe[0, 0]
    inverse_panel = panels[0, 0]
    primal_slots = primal_dofs[0, 0]
    flag_values = damage_flags[0, 0]
    width = loads_here.shape[2]
    primal_count = primal_slots.shape[0]
    positions = jnp.arange(4 * width, dtype=jnp.int32)
    picks = (primal_slots[:, None] == positions[None, :]).reshape(primal_count, 4, width)
    picks_half = picks.astype(jnp.bfloat16)
    picks_full = picks.astype(jnp.float32)
    flags_full = flag_values.astype(jnp.float32)

    def add_coarse(piece):
        return jnp.dot(coarse_inverse, piece.astype(jnp.float32), precision=lax.Precision.HIGHEST)

    def precondition(resid, schur_partner):
        scaled = face_mul_turned(resid.astype(jnp.bfloat16), deluxe_panel).astype(jnp.bfloat16)
        local_part = face_mul(scaled, inverse_panel)
        extra = face_mul(local_part.astype(jnp.bfloat16), inverse_panel)
        softened = lax.optimization_barrier(local_part + 0.5 * flags_full[:, None, None] * extra)
        primal = jnp.einsum(
            "kfx,frx->kr", picks_half, scaled, preferred_element_type=jnp.float32
        ).astype(jnp.bfloat16)
        coarse = add_coarse(gather_rows(primal, ("gx", "gy")))
        placed = jnp.einsum("kfx,kr->frx", picks_full, coarse, precision=lax.Precision.HIGHEST)
        weighted = (softened + placed).astype(jnp.bfloat16)
        spread = face_mul(weighted, deluxe_panel).astype(jnp.bfloat16)
        if schur_partner is not None:
            return spread.astype(jnp.float32) + face_pairs(spread).astype(jnp.float32), schur_partner
        received = jnp.stack(
            [
                from_partner(jnp.concatenate([spread[face], schur_panel[face]]), axis, from_lower)
                for axis, from_lower, face in PARTNERS
            ]
        )
        rows = spread.shape[1]
        spread_partner = received[:, :rows]
        return spread.astype(jnp.float32) + spread_partner.astype(jnp.float32), received[:, rows:]

    def apply_operator(field, schur_partner):
        field_half = field.astype(jnp.bfloat16)
        bent_own = to_half(face_mul(field_half, schur_panel))
        bent_partner = to_half(face_mul(field_half, schur_partner))
        return bent_own + bent_partner

    resid0 = loads_here.astype(jnp.float32) + face_pairs(loads_here).astype(jnp.float32)
    first, schur_partner = precondition(resid0, None)
    resid1 = resid0 - apply_operator(first, schur_partner)
    second, _ = precondition(resid1, schur_partner)
    curved = apply_operator(second, schur_partner)
    partial = jnp.stack(
        [jnp.sum(resid1 * second, axis=(0, 2)), jnp.sum(second * curved, axis=(0, 2))]
    )
    top, bottom = sum_over(partial, ("gx", "gy"))
    step_len = top / bottom
    result = (first + step_len[:, None] * second).astype(jnp.bfloat16)
    return result[None, None]


def solution(mesh):
    return jax.shard_map(
        per_device,
        mesh=mesh,
        in_specs=(
            P("gx", "gy", None, None, None),
            P("gx", "gy", None, None, None),
            P("gx", "gy", None, None, None),
            P("gx", "gy", None, None, None),
            P(("gx", "gy"), None),
            P("gx", "gy", None),
            P("gx", "gy", None),
        ),
        out_specs=P("gx", "gy", None, None, None),
        check_vma=False,
    )
```

```python
import jax
import jax.numpy as jnp
from jax import lax
from jax.sharding import PartitionSpec as P


def with_halo(block, sides, width):
    for axis, dim in sides:
        count = lax.axis_size(axis)
        forward = [(i, i + 1) for i in range(count - 1)]
        backward = [(target, source) for source, target in forward]
        low = lax.ppermute(
            lax.slice_in_dim(block, block.shape[dim] - width, None, axis=dim), axis, forward
        )
        high = lax.ppermute(lax.slice_in_dim(block, 0, width, axis=dim), axis, backward)
        block = jnp.concatenate([low, block, high], axis=dim)
    return block


def gather_rows(block, axes):
    count = lax.axis_size(axes)
    spread = jnp.broadcast_to(block[None], (count,) + block.shape)
    swapped = lax.all_to_all(spread, axes, 0, 0, tiled=False)
    return swapped.reshape((count * block.shape[0],) + block.shape[1:])


def sum_over(block, axes):
    return jnp.sum(gather_rows(block[None], axes), axis=0)


PARTNERS = (("gx", True, 1), ("gx", False, 0), ("gy", True, 3), ("gy", False, 2))


def from_partner(values, axis, from_lower):
    count = lax.axis_size(axis)
    if from_lower:
        pairs = [(i, i + 1) for i in range(count - 1)]
    else:
        pairs = [(i + 1, i) for i in range(count - 1)]
    return lax.ppermute(values, axis, pairs)


def to_half(values):
    return lax.reduce_precision(values, exponent_bits=8, mantissa_bits=7)


def face_mul(vectors, matrices):
    return jnp.einsum("fry,fyx->frx", vectors, matrices, preferred_element_type=jnp.float32)


def face_mul_turned(vectors, matrices):
    return jnp.einsum("fry,fxy->frx", vectors, matrices, preferred_element_type=jnp.float32)


def face_pairs(values):
    along_first = with_halo(values[0:2], (("gx", 0),), 1)
    along_second = with_halo(values[2:4], (("gy", 0),), 1)
    return jnp.stack([along_first[0], along_first[3], along_second[0], along_second[3]], axis=0)


def per_device(load_parts, schur, deluxe, panels, coarse_inverse, primal_dofs, damage_flags):
    loads_here = load_parts[0, 0]
    schur_panel = schur[0, 0]
    deluxe_panel = deluxe[0, 0]
    inverse_panel = panels[0, 0]
    primal_slots = primal_dofs[0, 0]
    flag_values = damage_flags[0, 0]
    width = loads_here.shape[2]
    primal_count = primal_slots.shape[0]
    positions = jnp.arange(4 * width, dtype=jnp.int32)
    picks = (primal_slots[:, None] == positions[None, :]).reshape(primal_count, 4, width)
    picks_half = picks.astype(jnp.bfloat16)
    picks_triple = jnp.concatenate([picks_half] * 3)
    flags_full = flag_values.astype(jnp.float32)

    def add_coarse(piece):
        return jnp.dot(coarse_inverse, piece.astype(jnp.float32), precision=lax.Precision.HIGHEST)

    def precondition(resid, schur_partner):
        scaled = face_mul_turned(resid.astype(jnp.bfloat16), deluxe_panel).astype(jnp.bfloat16)
        local_part = face_mul(scaled, inverse_panel)
        extra = face_mul(local_part.astype(jnp.bfloat16), inverse_panel)
        softened = lax.optimization_barrier(local_part + 0.5 * flags_full[:, None, None] * extra)
        primal = jnp.einsum(
            "kfx,frx->kr", picks_half, scaled, preferred_element_type=jnp.float32
        ).astype(jnp.bfloat16)
        coarse = add_coarse(gather_rows(primal, ("gx", "gy")))
        high = to_half(coarse)
        rest = coarse - high
        middle = to_half(rest)
        pieces = jnp.concatenate([high, middle, rest - middle]).astype(jnp.bfloat16)
        placed = jnp.einsum(
            "kfx,kr->frx", picks_triple, pieces, preferred_element_type=jnp.float32
        )
        weighted = (softened + placed).astype(jnp.bfloat16)
        spread = face_mul(weighted, deluxe_panel).astype(jnp.bfloat16)
        if schur_partner is not None:
            return spread.astype(jnp.float32) + face_pairs(spread).astype(jnp.float32), schur_partner
        received = jnp.stack(
            [
                from_partner(jnp.concatenate([spread[face], schur_panel[face]]), axis, from_lower)
                for axis, from_lower, face in PARTNERS
            ]
        )
        rows = spread.shape[1]
        spread_partner = received[:, :rows]
        return spread.astype(jnp.float32) + spread_partner.astype(jnp.float32), received[:, rows:]

    def apply_operator(field, schur_partner):
        field_half = field.astype(jnp.bfloat16)
        bent_own = to_half(face_mul(field_half, schur_panel))
        bent_partner = to_half(face_mul(field_half, schur_partner))
        return bent_own + bent_partner

    resid0 = loads_here.astype(jnp.float32) + face_pairs(loads_here).astype(jnp.float32)
    first, schur_partner = precondition(resid0, None)
    resid1 = resid0 - apply_operator(first, schur_partner)
    second, _ = precondition(resid1, schur_partner)
    curved = apply_operator(second, schur_partner)
    partial = jnp.stack(
        [jnp.sum(resid1 * second, axis=(0, 2)), jnp.sum(second * curved, axis=(0, 2))]
    )
    top, bottom = sum_over(partial, ("gx", "gy"))
    step_len = top / bottom
    result = (first + step_len[:, None] * second).astype(jnp.bfloat16)
    return result[None, None]


def solution(mesh):
    return jax.shard_map(
        per_device,
        mesh=mesh,
        in_specs=(
            P("gx", "gy", None, None, None),
            P("gx", "gy", None, None, None),
            P("gx", "gy", None, None, None),
            P("gx", "gy", None, None, None),
            P(("gx", "gy"), None),
            P("gx", "gy", None),
            P("gx", "gy", None),
        ),
        out_specs=P("gx", "gy", None, None, None),
        check_vma=False,
    )
```

```python
import jax
import jax.numpy as jnp
from jax import lax
from jax.sharding import PartitionSpec as P


def with_halo(block, sides, width):
    for axis, dim in sides:
        count = lax.axis_size(axis)
        forward = [(i, i + 1) for i in range(count - 1)]
        backward = [(target, source) for source, target in forward]
        low = lax.ppermute(
            lax.slice_in_dim(block, block.shape[dim] - width, None, axis=dim), axis, forward
        )
        high = lax.ppermute(lax.slice_in_dim(block, 0, width, axis=dim), axis, backward)
        block = jnp.concatenate([low, block, high], axis=dim)
    return block


def gather_rows(block, axes):
    count = lax.axis_size(axes)
    spread = jnp.broadcast_to(block[None], (count,) + block.shape)
    swapped = lax.all_to_all(spread, axes, 0, 0, tiled=False)
    return swapped.reshape((count * block.shape[0],) + block.shape[1:])


def sum_over(block, axes):
    return jnp.sum(gather_rows(block[None], axes), axis=0)


PARTNERS = (("gx", True, 1), ("gx", False, 0), ("gy", True, 3), ("gy", False, 2))


def from_partner(values, axis, from_lower):
    count = lax.axis_size(axis)
    if from_lower:
        pairs = [(i, i + 1) for i in range(count - 1)]
    else:
        pairs = [(i + 1, i) for i in range(count - 1)]
    return lax.ppermute(values, axis, pairs)


def to_half(values):
    return lax.reduce_precision(values, exponent_bits=8, mantissa_bits=7)


def face_mul(vectors, matrices):
    return jnp.einsum("fry,fyx->frx", vectors, matrices, preferred_element_type=jnp.float32)


def face_mul_turned(vectors, matrices):
    return jnp.einsum("fry,fxy->frx", vectors, matrices, preferred_element_type=jnp.float32)


def face_pairs(values):
    along_first = with_halo(values[0:2], (("gx", 0),), 1)
    along_second = with_halo(values[2:4], (("gy", 0),), 1)
    return jnp.stack([along_first[0], along_first[3], along_second[0], along_second[3]], axis=0)


def per_device(load_parts, schur, deluxe, panels, coarse_inverse, primal_dofs, damage_flags):
    loads_here = load_parts[0, 0]
    schur_panel = schur[0, 0]
    deluxe_panel = deluxe[0, 0]
    inverse_panel = panels[0, 0]
    primal_slots = primal_dofs[0, 0]
    flag_values = damage_flags[0, 0]
    width = loads_here.shape[2]
    primal_count = primal_slots.shape[0]
    positions = jnp.arange(4 * width, dtype=jnp.int32)
    picks = (primal_slots[:, None] == positions[None, :]).reshape(primal_count, 4, width)
    picks_half = picks.astype(jnp.bfloat16)
    picks_full = picks.astype(jnp.float32)
    flags_full = flag_values.astype(jnp.float32)

    def add_coarse(piece):
        return jnp.dot(coarse_inverse, piece.astype(jnp.float32), precision=lax.Precision.HIGHEST)

    def precondition(resid, schur_partner):
        scaled = face_mul_turned(resid.astype(jnp.bfloat16), deluxe_panel).astype(jnp.bfloat16)
        local_part = face_mul(scaled, inverse_panel)
        extra = face_mul(local_part.astype(jnp.bfloat16), inverse_panel)
        softened = lax.optimization_barrier(local_part + 0.5 * flags_full[:, None, None] * extra)
        primal = jnp.einsum(
            "kfx,frx->kr", picks_half, scaled, preferred_element_type=jnp.float32
        ).astype(jnp.bfloat16)
        coarse = add_coarse(gather_rows(primal, ("gx", "gy")))
        placed = jnp.einsum("kfx,kr->frx", picks_full, coarse, precision=lax.Precision.HIGHEST)
        weighted = (softened + placed).astype(jnp.bfloat16)
        spread = face_mul(weighted, deluxe_panel).astype(jnp.bfloat16)
        if schur_partner is not None:
            return spread.astype(jnp.float32) + face_pairs(spread).astype(jnp.float32), schur_partner
        received = jnp.stack(
            [
                from_partner(jnp.concatenate([spread[face], schur_panel[face]]), axis, from_lower)
                for axis, from_lower, face in PARTNERS
            ]
        )
        rows = spread.shape[1]
        spread_partner = received[:, :rows]
        return spread.astype(jnp.float32) + spread_partner.astype(jnp.float32), received[:, rows:]

    def apply_operator(field, schur_partner):
        field_half = field.astype(jnp.bfloat16)
        bent_own = to_half(face_mul(field_half, schur_panel))
        bent_partner = to_half(face_mul(field_half, schur_partner))
        return bent_own + bent_partner

    load_partner = jnp.stack(
        [from_partner(loads_here[face], axis, from_lower) for axis, from_lower, face in PARTNERS]
    )
    resid0 = loads_here.astype(jnp.float32) + load_partner.astype(jnp.float32)
    first, schur_partner = precondition(resid0, None)
    resid1 = resid0 - apply_operator(first, schur_partner)
    second, _ = precondition(resid1, schur_partner)
    curved = apply_operator(second, schur_partner)
    partial = jnp.stack(
        [jnp.sum(resid1 * second, axis=(0, 2)), jnp.sum(second * curved, axis=(0, 2))]
    )
    top, bottom = sum_over(partial, ("gx", "gy"))
    step_len = top / bottom
    result = (first + step_len[:, None] * second).astype(jnp.bfloat16)
    return result[None, None]


def solution(mesh):
    return jax.shard_map(
        per_device,
        mesh=mesh,
        in_specs=(
            P("gx", "gy", None, None, None),
            P("gx", "gy", None, None, None),
            P("gx", "gy", None, None, None),
            P("gx", "gy", None, None, None),
            P(("gx", "gy"), None),
            P("gx", "gy", None),
            P("gx", "gy", None),
        ),
        out_specs=P("gx", "gy", None, None, None),
        check_vma=False,
    )
```

```python
import jax
import jax.numpy as jnp
from jax import lax
from jax.sharding import PartitionSpec as P


def with_halo(block, sides, width):
    for axis, dim in sides:
        count = lax.axis_size(axis)
        forward = [(i, i + 1) for i in range(count - 1)]
        backward = [(target, source) for source, target in forward]
        low = lax.ppermute(
            lax.slice_in_dim(block, block.shape[dim] - width, None, axis=dim), axis, forward
        )
        high = lax.ppermute(lax.slice_in_dim(block, 0, width, axis=dim), axis, backward)
        block = jnp.concatenate([low, block, high], axis=dim)
    return block


def gather_rows(block, axes):
    count = lax.axis_size(axes)
    spread = jnp.broadcast_to(block[None], (count,) + block.shape)
    swapped = lax.all_to_all(spread, axes, 0, 0, tiled=False)
    return swapped.reshape((count * block.shape[0],) + block.shape[1:])


def sum_over(block, axes):
    return jnp.sum(gather_rows(block[None], axes), axis=0)


PARTNERS = (("gx", True, 1), ("gx", False, 0), ("gy", True, 3), ("gy", False, 2))


def from_partner(values, axis, from_lower):
    count = lax.axis_size(axis)
    if from_lower:
        pairs = [(i, i + 1) for i in range(count - 1)]
    else:
        pairs = [(i + 1, i) for i in range(count - 1)]
    return lax.ppermute(values, axis, pairs)


def to_half(values):
    return lax.reduce_precision(values, exponent_bits=8, mantissa_bits=7)


def face_mul(vectors, matrices):
    return jnp.einsum("fry,fyx->frx", vectors, matrices, preferred_element_type=jnp.float32)


def face_mul_turned(vectors, matrices):
    return jnp.einsum("fry,fxy->frx", vectors, matrices, preferred_element_type=jnp.float32)


def face_pairs(values):
    along_first = with_halo(values[0:2], (("gx", 0),), 1)
    along_second = with_halo(values[2:4], (("gy", 0),), 1)
    return jnp.stack([along_first[0], along_first[3], along_second[0], along_second[3]], axis=0)


def per_device(load_parts, schur, deluxe, panels, coarse_inverse, primal_dofs, damage_flags):
    loads_here = load_parts[0, 0]
    schur_panel = schur[0, 0]
    deluxe_panel = deluxe[0, 0]
    inverse_panel = panels[0, 0]
    primal_slots = primal_dofs[0, 0]
    flag_values = damage_flags[0, 0]
    width = loads_here.shape[2]
    primal_count = primal_slots.shape[0]
    positions = jnp.arange(4 * width, dtype=jnp.int32)
    picks = (primal_slots[:, None] == positions[None, :]).reshape(primal_count, 4, width)
    picks_half = picks.astype(jnp.bfloat16)
    picks_full = picks.astype(jnp.float32)
    flags_full = flag_values.astype(jnp.float32)

    def add_coarse(rows, piece):
        return jnp.dot(rows, piece, precision=lax.Precision.HIGHEST)

    rows = loads_here.shape[1]
    coarse_width = coarse_inverse.shape[1]
    small = jnp.concatenate(
        [
            coarse_inverse,
            jnp.pad(
                jnp.concatenate([primal_slots, flag_values]).astype(jnp.float32)[None],
                ((0, 0), (0, coarse_width - 2 * primal_count)),
            ),
        ]
    )
    halo, small_y = [], []
    for axis, from_lower, face in PARTNERS:
        payload = loads_here[face]
        if axis == "gy":
            payload = jnp.concatenate(
                [payload, deluxe_panel[face], inverse_panel[face], schur_panel[face]]
            )
            small_y.append(from_partner(small, axis, from_lower))
        halo.append(from_partner(payload, axis, from_lower))
    load_partner = jnp.stack([received[:rows] for received in halo])
    mats_y = jnp.stack([received[rows:].reshape(3, width, width) for received in halo[2:]])
    deluxe_y, panels_y, schur_y = mats_y[:, 0], mats_y[:, 1], mats_y[:, 2]
    small_y = jnp.stack(small_y)
    rows_y = small_y[:, :primal_count].reshape(-1, coarse_width)
    slots_y = small_y[:, primal_count, :primal_count].astype(jnp.int32)
    flags_y = jnp.stack(
        [small_y[p, primal_count, primal_count + face] for p, (_, _, face) in enumerate(PARTNERS[2:])]
    )
    offsets_y = jnp.array([face * width for _, _, face in PARTNERS[2:]], jnp.int32)
    picks_y = (
        slots_y[:, :, None]
        == (offsets_y[:, None, None] + jnp.arange(width, dtype=jnp.int32)[None, None, :])
    ).astype(jnp.float32)

    def softened_of(resid_half, deluxe_faces, panels_faces, flags):
        scaled = face_mul_turned(resid_half, deluxe_faces).astype(jnp.bfloat16)
        local_part = face_mul(scaled, panels_faces)
        extra = face_mul(local_part.astype(jnp.bfloat16), panels_faces)
        return scaled, lax.optimization_barrier(local_part + 0.5 * flags[:, None, None] * extra)

    def precondition(resid, schur_x):
        resid_half = resid.astype(jnp.bfloat16)
        scaled, softened = softened_of(resid_half, deluxe_panel, inverse_panel, flags_full)
        _, softened_y = softened_of(resid_half[2:4], deluxe_y, panels_y, flags_y)
        primal = jnp.einsum(
            "kfx,frx->kr", picks_half, scaled, preferred_element_type=jnp.float32
        ).astype(jnp.bfloat16)
        primal_all = gather_rows(primal, ("gx", "gy")).astype(jnp.float32)
        coarse = add_coarse(coarse_inverse, primal_all)
        coarse_y = add_coarse(rows_y, primal_all).reshape(2, primal_count, -1)
        placed = jnp.einsum("kfx,kr->frx", picks_full, coarse, precision=lax.Precision.HIGHEST)
        placed_y = jnp.einsum("pkx,pkr->prx", picks_y, coarse_y, precision=lax.Precision.HIGHEST)
        weighted = (softened + placed).astype(jnp.bfloat16)
        weighted_y = (softened_y + placed_y).astype(jnp.bfloat16)
        spread = face_mul(weighted, deluxe_panel).astype(jnp.bfloat16)
        spread_y = to_half(face_mul(weighted_y, deluxe_y))
        received = []
        for axis, from_lower, face in PARTNERS[:2]:
            payload = spread[face]
            if schur_x is None:
                payload = jnp.concatenate([payload, schur_panel[face]])
            received.append(from_partner(payload, axis, from_lower))
        received = jnp.stack(received)
        if schur_x is None:
            schur_x = received[:, rows:]
        partner = jnp.concatenate([received[:, :rows].astype(jnp.float32), spread_y])
        return spread.astype(jnp.float32) + partner, schur_x

    def apply_operator(field, schur_partner):
        field_half = field.astype(jnp.bfloat16)
        bent_own = to_half(face_mul(field_half, schur_panel))
        bent_partner = to_half(face_mul(field_half, schur_partner))
        return bent_own + bent_partner

    resid0 = loads_here.astype(jnp.float32) + load_partner.astype(jnp.float32)
    first, schur_x = precondition(resid0, None)
    schur_partner = jnp.concatenate([schur_x, schur_y])
    resid1 = resid0 - apply_operator(first, schur_partner)
    second, _ = precondition(resid1, schur_x)
    curved = apply_operator(second, schur_partner)
    partial = jnp.stack(
        [jnp.sum(resid1 * second, axis=(0, 2)), jnp.sum(second * curved, axis=(0, 2))]
    )
    top, bottom = sum_over(partial, ("gx", "gy"))
    step_len = top / bottom
    result = (first + step_len[:, None] * second).astype(jnp.bfloat16)
    return result[None, None]


def solution(mesh):
    return jax.shard_map(
        per_device,
        mesh=mesh,
        in_specs=(
            P("gx", "gy", None, None, None),
            P("gx", "gy", None, None, None),
            P("gx", "gy", None, None, None),
            P("gx", "gy", None, None, None),
            P(("gx", "gy"), None),
            P("gx", "gy", None),
            P("gx", "gy", None),
        ),
        out_specs=P("gx", "gy", None, None, None),
        check_vma=False,
    )
```

```python
import jax
import jax.numpy as jnp
from jax import lax
from jax.sharding import PartitionSpec as P


def with_halo(block, sides, width):
    for axis, dim in sides:
        count = lax.axis_size(axis)
        forward = [(i, i + 1) for i in range(count - 1)]
        backward = [(target, source) for source, target in forward]
        low = lax.ppermute(
            lax.slice_in_dim(block, block.shape[dim] - width, None, axis=dim), axis, forward
        )
        high = lax.ppermute(lax.slice_in_dim(block, 0, width, axis=dim), axis, backward)
        block = jnp.concatenate([low, block, high], axis=dim)
    return block


def gather_rows(block, axes):
    count = lax.axis_size(axes)
    spread = jnp.broadcast_to(block[None], (count,) + block.shape)
    swapped = lax.all_to_all(spread, axes, 0, 0, tiled=False)
    return swapped.reshape((count * block.shape[0],) + block.shape[1:])


def sum_over(block, axes):
    return jnp.sum(gather_rows(block[None], axes), axis=0)


PARTNERS = (("gx", True, 1), ("gx", False, 0), ("gy", True, 3), ("gy", False, 2))


def from_partner(values, axis, from_lower):
    count = lax.axis_size(axis)
    if from_lower:
        pairs = [(i, i + 1) for i in range(count - 1)]
    else:
        pairs = [(i + 1, i) for i in range(count - 1)]
    return lax.ppermute(values, axis, pairs)


def to_half(values):
    return lax.reduce_precision(values, exponent_bits=8, mantissa_bits=7)


def face_mul(vectors, matrices):
    return jnp.einsum("fry,fyx->frx", vectors, matrices, preferred_element_type=jnp.float32)


def face_mul_turned(vectors, matrices):
    return jnp.einsum("fry,fxy->frx", vectors, matrices, preferred_element_type=jnp.float32)


def face_pairs(values):
    along_first = with_halo(values[0:2], (("gx", 0),), 1)
    along_second = with_halo(values[2:4], (("gy", 0),), 1)
    return jnp.stack([along_first[0], along_first[3], along_second[0], along_second[3]], axis=0)


def per_device(load_parts, schur, deluxe, panels, coarse_inverse, primal_dofs, damage_flags):
    loads_here = load_parts[0, 0]
    schur_panel = schur[0, 0]
    deluxe_panel = deluxe[0, 0]
    inverse_panel = panels[0, 0]
    primal_slots = primal_dofs[0, 0]
    flag_values = damage_flags[0, 0]
    width = loads_here.shape[2]
    primal_count = primal_slots.shape[0]
    positions = jnp.arange(4 * width, dtype=jnp.int32)
    picks = (primal_slots[:, None] == positions[None, :]).reshape(primal_count, 4, width)
    picks_half = picks.astype(jnp.bfloat16)
    picks_full = picks.astype(jnp.float32)
    flags_full = flag_values.astype(jnp.float32)

    def add_coarse(piece):
        return jnp.dot(coarse_inverse, piece.astype(jnp.float32), precision=lax.Precision.HIGHEST)

    def precondition(resid, schur_partner):
        scaled = face_mul_turned(resid.astype(jnp.bfloat16), deluxe_panel).astype(jnp.bfloat16)
        local_part = face_mul(scaled, inverse_panel)
        extra = face_mul(local_part.astype(jnp.bfloat16), inverse_panel)
        softened = lax.optimization_barrier(local_part + 0.5 * flags_full[:, None, None] * extra)
        primal = jnp.einsum(
            "kfx,frx->kr", picks_half, scaled, preferred_element_type=jnp.float32
        ).astype(jnp.bfloat16)
        if schur_partner is None:
            schur_source, primal = lax.optimization_barrier((schur_panel[0:2], primal))
            schur_x = jnp.stack(
                [
                    from_partner(schur_source[face], axis, from_lower)
                    for axis, from_lower, face in PARTNERS[:2]
                ]
            )
        coarse = add_coarse(gather_rows(primal, ("gx", "gy")))
        placed = jnp.einsum("kfx,kr->frx", picks_full, coarse, precision=lax.Precision.HIGHEST)
        weighted = (softened + placed).astype(jnp.bfloat16)
        if schur_partner is None:
            schur_x, weighted = lax.optimization_barrier((schur_x, weighted))
        spread = face_mul(weighted, deluxe_panel).astype(jnp.bfloat16)
        if schur_partner is not None:
            return spread.astype(jnp.float32) + face_pairs(spread).astype(jnp.float32), schur_partner
        rows = spread.shape[1]
        received_x = jnp.stack(
            [from_partner(spread[face], axis, from_lower) for axis, from_lower, face in PARTNERS[:2]]
        )
        received_y = jnp.stack(
            [
                from_partner(jnp.concatenate([spread[face], schur_panel[face]]), axis, from_lower)
                for axis, from_lower, face in PARTNERS[2:]
            ]
        )
        spread_partner = jnp.concatenate([received_x, received_y[:, :rows]])
        schur_partner = jnp.concatenate([schur_x, received_y[:, rows:]])
        return spread.astype(jnp.float32) + spread_partner.astype(jnp.float32), schur_partner

    def apply_operator(field, schur_partner):
        field_half = field.astype(jnp.bfloat16)
        bent_own = to_half(face_mul(field_half, schur_panel))
        bent_partner = to_half(face_mul(field_half, schur_partner))
        return bent_own + bent_partner

    resid0 = loads_here.astype(jnp.float32) + face_pairs(loads_here).astype(jnp.float32)
    first, schur_partner = precondition(resid0, None)
    resid1 = resid0 - apply_operator(first, schur_partner)
    second, _ = precondition(resid1, schur_partner)
    curved = apply_operator(second, schur_partner)
    partial = jnp.stack(
        [jnp.sum(resid1 * second, axis=(0, 2)), jnp.sum(second * curved, axis=(0, 2))]
    )
    top, bottom = sum_over(partial, ("gx", "gy"))
    step_len = top / bottom
    result = (first + step_len[:, None] * second).astype(jnp.bfloat16)
    return result[None, None]


def solution(mesh):
    return jax.shard_map(
        per_device,
        mesh=mesh,
        in_specs=(
            P("gx", "gy", None, None, None),
            P("gx", "gy", None, None, None),
            P("gx", "gy", None, None, None),
            P("gx", "gy", None, None, None),
            P(("gx", "gy"), None),
            P("gx", "gy", None),
            P("gx", "gy", None),
        ),
        out_specs=P("gx", "gy", None, None, None),
        check_vma=False,
    )
```

```python
import jax
import jax.numpy as jnp
from jax import lax
from jax.sharding import PartitionSpec as P


def with_halo(block, sides, width):
    for axis, dim in sides:
        count = lax.axis_size(axis)
        forward = [(i, i + 1) for i in range(count - 1)]
        backward = [(target, source) for source, target in forward]
        low = lax.ppermute(
            lax.slice_in_dim(block, block.shape[dim] - width, None, axis=dim), axis, forward
        )
        high = lax.ppermute(lax.slice_in_dim(block, 0, width, axis=dim), axis, backward)
        block = jnp.concatenate([low, block, high], axis=dim)
    return block


def gather_rows(block, axes):
    count = lax.axis_size(axes)
    spread = jnp.broadcast_to(block[None], (count,) + block.shape)
    swapped = lax.all_to_all(spread, axes, 0, 0, tiled=False)
    return swapped.reshape((count * block.shape[0],) + block.shape[1:])


def sum_over(block, axes):
    return jnp.sum(gather_rows(block[None], axes), axis=0)


PARTNERS = (("gx", True, 1), ("gx", False, 0), ("gy", True, 3), ("gy", False, 2))


def from_partner(values, axis, from_lower):
    count = lax.axis_size(axis)
    if from_lower:
        pairs = [(i, i + 1) for i in range(count - 1)]
    else:
        pairs = [(i + 1, i) for i in range(count - 1)]
    return lax.ppermute(values, axis, pairs)


def to_half(values):
    return lax.reduce_precision(values, exponent_bits=8, mantissa_bits=7)


def face_mul(vectors, matrices):
    return jnp.einsum("fry,fyx->frx", vectors, matrices, preferred_element_type=jnp.float32)


def face_mul_turned(vectors, matrices):
    return jnp.einsum("fry,fxy->frx", vectors, matrices, preferred_element_type=jnp.float32)


def face_pairs(values):
    along_first = with_halo(values[0:2], (("gx", 0),), 1)
    along_second = with_halo(values[2:4], (("gy", 0),), 1)
    return jnp.stack([along_first[0], along_first[3], along_second[0], along_second[3]], axis=0)


def per_device(load_parts, schur, deluxe, panels, coarse_inverse, primal_dofs, damage_flags):
    loads_here = load_parts[0, 0]
    schur_panel = schur[0, 0]
    deluxe_panel = deluxe[0, 0]
    inverse_panel = panels[0, 0]
    primal_slots = primal_dofs[0, 0]
    flag_values = damage_flags[0, 0]
    width = loads_here.shape[2]
    primal_count = primal_slots.shape[0]
    positions = jnp.arange(4 * width, dtype=jnp.int32)
    picks = (primal_slots[:, None] == positions[None, :]).reshape(primal_count, 4, width)
    picks_half = picks.astype(jnp.bfloat16)
    picks_full = picks.astype(jnp.float32)
    flags_full = flag_values.astype(jnp.float32)

    padded_count = 8
    devices = coarse_inverse.shape[1] // primal_count
    coarse_padded = jnp.pad(
        coarse_inverse.reshape(primal_count, devices, primal_count),
        ((0, 0), (0, 0), (0, padded_count - primal_count)),
    ).reshape(primal_count, devices * padded_count)

    def add_coarse(piece):
        return jnp.dot(coarse_padded, piece.astype(jnp.float32), precision=lax.Precision.HIGHEST)

    def precondition(resid, schur_partner):
        scaled = face_mul_turned(resid.astype(jnp.bfloat16), deluxe_panel).astype(jnp.bfloat16)
        local_part = face_mul(scaled, inverse_panel)
        extra = face_mul(local_part.astype(jnp.bfloat16), inverse_panel)
        softened = lax.optimization_barrier(local_part + 0.5 * flags_full[:, None, None] * extra)
        primal = jnp.einsum(
            "kfx,frx->kr", picks_half, scaled, preferred_element_type=jnp.float32
        ).astype(jnp.bfloat16)
        coarse = add_coarse(
            gather_rows(jnp.pad(primal, ((0, padded_count - primal_count), (0, 0))), ("gx", "gy"))
        )
        placed = jnp.einsum("kfx,kr->frx", picks_full, coarse, precision=lax.Precision.HIGHEST)
        weighted = (softened + placed).astype(jnp.bfloat16)
        spread = face_mul(weighted, deluxe_panel).astype(jnp.bfloat16)
        if schur_partner is not None:
            return spread.astype(jnp.float32) + face_pairs(spread).astype(jnp.float32), schur_partner
        received = jnp.stack(
            [
                from_partner(jnp.concatenate([spread[face], schur_panel[face]]), axis, from_lower)
                for axis, from_lower, face in PARTNERS
            ]
        )
        rows = spread.shape[1]
        spread_partner = received[:, :rows]
        return spread.astype(jnp.float32) + spread_partner.astype(jnp.float32), received[:, rows:]

    def apply_operator(field, schur_partner):
        field_half = field.astype(jnp.bfloat16)
        bent_own = to_half(face_mul(field_half, schur_panel))
        bent_partner = to_half(face_mul(field_half, schur_partner))
        return bent_own + bent_partner

    resid0 = loads_here.astype(jnp.float32) + face_pairs(loads_here).astype(jnp.float32)
    first, schur_partner = precondition(resid0, None)
    resid1 = resid0 - apply_operator(first, schur_partner)
    second, _ = precondition(resid1, schur_partner)
    curved = apply_operator(second, schur_partner)
    partial = jnp.stack(
        [jnp.sum(resid1 * second, axis=(0, 2)), jnp.sum(second * curved, axis=(0, 2))]
    )
    top, bottom = sum_over(partial, ("gx", "gy"))
    step_len = top / bottom
    result = (first + step_len[:, None] * second).astype(jnp.bfloat16)
    return result[None, None]


def solution(mesh):
    return jax.shard_map(
        per_device,
        mesh=mesh,
        in_specs=(
            P("gx", "gy", None, None, None),
            P("gx", "gy", None, None, None),
            P("gx", "gy", None, None, None),
            P("gx", "gy", None, None, None),
            P(("gx", "gy"), None),
            P("gx", "gy", None),
            P("gx", "gy", None),
        ),
        out_specs=P("gx", "gy", None, None, None),
        check_vma=False,
    )
```

```python
import jax
import jax.numpy as jnp
from jax import lax
from jax.experimental import pallas as pl
from jax.sharding import PartitionSpec as P


def with_halo(block, sides, width):
    for axis, dim in sides:
        count = lax.axis_size(axis)
        forward = [(i, i + 1) for i in range(count - 1)]
        backward = [(target, source) for source, target in forward]
        low = lax.ppermute(
            lax.slice_in_dim(block, block.shape[dim] - width, None, axis=dim), axis, forward
        )
        high = lax.ppermute(lax.slice_in_dim(block, 0, width, axis=dim), axis, backward)
        block = jnp.concatenate([low, block, high], axis=dim)
    return block


def gather_rows(block, axes):
    count = lax.axis_size(axes)
    spread = jnp.broadcast_to(block[None], (count,) + block.shape)
    swapped = lax.all_to_all(spread, axes, 0, 0, tiled=False)
    return swapped.reshape((count * block.shape[0],) + block.shape[1:])


def sum_over(block, axes):
    return jnp.sum(gather_rows(block[None], axes), axis=0)


PARTNERS = (("gx", True, 1), ("gx", False, 0), ("gy", True, 3), ("gy", False, 2))


def from_partner(values, axis, from_lower):
    count = lax.axis_size(axis)
    if from_lower:
        pairs = [(i, i + 1) for i in range(count - 1)]
    else:
        pairs = [(i + 1, i) for i in range(count - 1)]
    return lax.ppermute(values, axis, pairs)


def to_half(values):
    return lax.reduce_precision(values, exponent_bits=8, mantissa_bits=7)


def face_mul(vectors, matrices):
    return jnp.einsum("fry,fyx->frx", vectors, matrices, preferred_element_type=jnp.float32)


def face_mul_turned(vectors, matrices):
    return jnp.einsum("fry,fxy->frx", vectors, matrices, preferred_element_type=jnp.float32)


def soften_kernel(scaled_ref, panels_ref, flags_ref, out_ref):
    local_part = jnp.dot(scaled_ref[0], panels_ref[0], preferred_element_type=jnp.float32)
    extra = jnp.dot(
        local_part.astype(jnp.bfloat16), panels_ref[0], preferred_element_type=jnp.float32
    )
    out_ref[0] = local_part + flags_ref[0, 0:1, 0:1] * extra


def soften(scaled, panels, half_flags):
    faces, rows, width = scaled.shape
    flags = jnp.broadcast_to(half_flags[:, None, None], (faces, 8, 128))
    return pl.pallas_call(
        soften_kernel,
        grid=(faces,),
        in_specs=[
            pl.BlockSpec((1, rows, width), lambda f: (f, 0, 0)),
            pl.BlockSpec((1, width, width), lambda f: (f, 0, 0)),
            pl.BlockSpec((1, 8, 128), lambda f: (f, 0, 0)),
        ],
        out_specs=pl.BlockSpec((1, rows, width), lambda f: (f, 0, 0)),
        out_shape=jax.ShapeDtypeStruct((faces, rows, width), jnp.float32),
        cost_estimate=pl.CostEstimate(
            flops=4 * faces * rows * width * width,
            transcendentals=0,
            bytes_accessed=faces * (rows * width * 6 + width * width * 2),
        ),
    )(scaled, panels, flags)


def face_pairs(values):
    along_first = with_halo(values[0:2], (("gx", 0),), 1)
    along_second = with_halo(values[2:4], (("gy", 0),), 1)
    return jnp.stack([along_first[0], along_first[3], along_second[0], along_second[3]], axis=0)


def per_device(load_parts, schur, deluxe, panels, coarse_inverse, primal_dofs, damage_flags):
    loads_here = load_parts[0, 0]
    schur_panel = schur[0, 0]
    deluxe_panel = deluxe[0, 0]
    inverse_panel = panels[0, 0]
    primal_slots = primal_dofs[0, 0]
    flag_values = damage_flags[0, 0]
    width = loads_here.shape[2]
    primal_count = primal_slots.shape[0]
    positions = jnp.arange(4 * width, dtype=jnp.int32)
    picks = (primal_slots[:, None] == positions[None, :]).reshape(primal_count, 4, width)
    picks_half = picks.astype(jnp.bfloat16)
    picks_full = picks.astype(jnp.float32)
    flags_full = flag_values.astype(jnp.float32)

    def add_coarse(piece):
        return jnp.dot(coarse_inverse, piece.astype(jnp.float32), precision=lax.Precision.HIGHEST)

    def precondition(resid, schur_partner):
        scaled = face_mul_turned(resid.astype(jnp.bfloat16), deluxe_panel).astype(jnp.bfloat16)
        softened = soften(scaled, inverse_panel, 0.5 * flags_full)
        primal = jnp.einsum(
            "kfx,frx->kr", picks_half, scaled, preferred_element_type=jnp.float32
        ).astype(jnp.bfloat16)
        coarse = add_coarse(gather_rows(primal, ("gx", "gy")))
        placed = jnp.einsum("kfx,kr->frx", picks_full, coarse, precision=lax.Precision.HIGHEST)
        weighted = (softened + placed).astype(jnp.bfloat16)
        spread = face_mul(weighted, deluxe_panel).astype(jnp.bfloat16)
        if schur_partner is not None:
            return spread.astype(jnp.float32) + face_pairs(spread).astype(jnp.float32), schur_partner
        received = jnp.stack(
            [
                from_partner(jnp.concatenate([spread[face], schur_panel[face]]), axis, from_lower)
                for axis, from_lower, face in PARTNERS
            ]
        )
        rows = spread.shape[1]
        spread_partner = received[:, :rows]
        return spread.astype(jnp.float32) + spread_partner.astype(jnp.float32), received[:, rows:]

    def apply_operator(field, schur_partner):
        field_half = field.astype(jnp.bfloat16)
        bent_own = to_half(face_mul(field_half, schur_panel))
        bent_partner = to_half(face_mul(field_half, schur_partner))
        return bent_own + bent_partner

    resid0 = loads_here.astype(jnp.float32) + face_pairs(loads_here).astype(jnp.float32)
    first, schur_partner = precondition(resid0, None)
    resid1 = resid0 - apply_operator(first, schur_partner)
    second, _ = precondition(resid1, schur_partner)
    curved = apply_operator(second, schur_partner)
    partial = jnp.stack(
        [jnp.sum(resid1 * second, axis=(0, 2)), jnp.sum(second * curved, axis=(0, 2))]
    )
    top, bottom = sum_over(partial, ("gx", "gy"))
    step_len = top / bottom
    result = (first + step_len[:, None] * second).astype(jnp.bfloat16)
    return result[None, None]


def solution(mesh):
    return jax.shard_map(
        per_device,
        mesh=mesh,
        in_specs=(
            P("gx", "gy", None, None, None),
            P("gx", "gy", None, None, None),
            P("gx", "gy", None, None, None),
            P("gx", "gy", None, None, None),
            P(("gx", "gy"), None),
            P("gx", "gy", None),
            P("gx", "gy", None),
        ),
        out_specs=P("gx", "gy", None, None, None),
        check_vma=False,
    )
```

```python
import jax
import jax.numpy as jnp
from jax import lax
from jax.experimental import pallas as pl
from jax.sharding import PartitionSpec as P


def with_halo(block, sides, width):
    for axis, dim in sides:
        count = lax.axis_size(axis)
        forward = [(i, i + 1) for i in range(count - 1)]
        backward = [(target, source) for source, target in forward]
        low = lax.ppermute(
            lax.slice_in_dim(block, block.shape[dim] - width, None, axis=dim), axis, forward
        )
        high = lax.ppermute(lax.slice_in_dim(block, 0, width, axis=dim), axis, backward)
        block = jnp.concatenate([low, block, high], axis=dim)
    return block


def gather_rows(block, axes):
    count = lax.axis_size(axes)
    spread = jnp.broadcast_to(block[None], (count,) + block.shape)
    swapped = lax.all_to_all(spread, axes, 0, 0, tiled=False)
    return swapped.reshape((count * block.shape[0],) + block.shape[1:])


def sum_over(block, axes):
    return jnp.sum(gather_rows(block[None], axes), axis=0)


PARTNERS = (("gx", True, 1), ("gx", False, 0), ("gy", True, 3), ("gy", False, 2))


def from_partner(values, axis, from_lower):
    count = lax.axis_size(axis)
    if from_lower:
        pairs = [(i, i + 1) for i in range(count - 1)]
    else:
        pairs = [(i + 1, i) for i in range(count - 1)]
    return lax.ppermute(values, axis, pairs)


def to_half(values):
    return lax.reduce_precision(values, exponent_bits=8, mantissa_bits=7)


def face_mul(vectors, matrices):
    return jnp.einsum("fry,fyx->frx", vectors, matrices, preferred_element_type=jnp.float32)


def face_mul_turned(vectors, matrices):
    return jnp.einsum("fry,fxy->frx", vectors, matrices, preferred_element_type=jnp.float32)


def soften_kernel(scaled_ref, panels_ref, flags_ref, out_ref):
    local_part = jnp.dot(scaled_ref[0], panels_ref[0], preferred_element_type=jnp.float32)
    extra = jnp.dot(
        local_part.astype(jnp.bfloat16), panels_ref[0], preferred_element_type=jnp.float32
    )
    out_ref[0] = local_part + flags_ref[0, 0:1, 0:1] * extra


def soften(scaled, panels, half_flags):
    faces, rows, width = scaled.shape
    flags = jnp.broadcast_to(half_flags[:, None, None], (faces, 8, 128))
    return pl.pallas_call(
        soften_kernel,
        grid=(faces,),
        in_specs=[
            pl.BlockSpec((1, rows, width), lambda f: (f, 0, 0)),
            pl.BlockSpec((1, width, width), lambda f: (f, 0, 0)),
            pl.BlockSpec((1, 8, 128), lambda f: (f, 0, 0)),
        ],
        out_specs=pl.BlockSpec((1, rows, width), lambda f: (f, 0, 0)),
        out_shape=jax.ShapeDtypeStruct((faces, rows, width), jnp.float32),
        cost_estimate=pl.CostEstimate(
            flops=4 * faces * rows * width * width,
            transcendentals=0,
            bytes_accessed=faces * (rows * width * 6 + width * width * 2),
        ),
    )(scaled, panels, flags)


def spread_kernel(softened_ref, coarse_ref, slots_ref, deluxe_ref, out_ref):
    face = pl.program_id(0)
    rows, width = softened_ref.shape[1], softened_ref.shape[2]
    position = lax.broadcasted_iota(jnp.int32, (1, width), 1) + face * width
    placed = jnp.zeros((rows, width), jnp.float32)
    for k in range(coarse_ref.shape[1]):
        hit = slots_ref[0:1, k:k + 1] == position
        placed = placed + jnp.where(hit, coarse_ref[:, k:k + 1], 0.0)
    weighted = (softened_ref[0] + placed).astype(jnp.bfloat16)
    out_ref[0] = jnp.dot(
        weighted, deluxe_ref[0], preferred_element_type=jnp.float32
    ).astype(out_ref.dtype)


def spread_of(softened, coarse, slots_block, deluxe):
    faces, rows, width = softened.shape
    count = coarse.shape[0]
    return pl.pallas_call(
        spread_kernel,
        grid=(faces,),
        in_specs=[
            pl.BlockSpec((1, rows, width), lambda f: (f, 0, 0)),
            pl.BlockSpec((rows, count), lambda f: (0, 0)),
            pl.BlockSpec(slots_block.shape, lambda f: (0, 0)),
            pl.BlockSpec((1, width, width), lambda f: (f, 0, 0)),
        ],
        out_specs=pl.BlockSpec((1, rows, width), lambda f: (f, 0, 0)),
        out_shape=jax.ShapeDtypeStruct((faces, rows, width), jnp.bfloat16),
        cost_estimate=pl.CostEstimate(
            flops=2 * faces * rows * width * width,
            transcendentals=0,
            bytes_accessed=faces * (rows * width * 6 + width * width * 2),
        ),
    )(softened, coarse.T, slots_block, deluxe)


def face_pairs(values):
    along_first = with_halo(values[0:2], (("gx", 0),), 1)
    along_second = with_halo(values[2:4], (("gy", 0),), 1)
    return jnp.stack([along_first[0], along_first[3], along_second[0], along_second[3]], axis=0)


def per_device(load_parts, schur, deluxe, panels, coarse_inverse, primal_dofs, damage_flags):
    loads_here = load_parts[0, 0]
    schur_panel = schur[0, 0]
    deluxe_panel = deluxe[0, 0]
    inverse_panel = panels[0, 0]
    primal_slots = primal_dofs[0, 0]
    flag_values = damage_flags[0, 0]
    width = loads_here.shape[2]
    primal_count = primal_slots.shape[0]
    positions = jnp.arange(4 * width, dtype=jnp.int32)
    picks = (primal_slots[:, None] == positions[None, :]).reshape(primal_count, 4, width)
    picks_half = picks.astype(jnp.bfloat16)
    slots_block = jnp.zeros((8, 128), jnp.int32).at[0, :primal_count].set(primal_slots)
    flags_full = flag_values.astype(jnp.float32)

    def add_coarse(piece):
        return jnp.dot(coarse_inverse, piece.astype(jnp.float32), precision=lax.Precision.HIGHEST)

    def precondition(resid, schur_partner):
        scaled = face_mul_turned(resid.astype(jnp.bfloat16), deluxe_panel).astype(jnp.bfloat16)
        softened = soften(scaled, inverse_panel, 0.5 * flags_full)
        primal = jnp.einsum(
            "kfx,frx->kr", picks_half, scaled, preferred_element_type=jnp.float32
        ).astype(jnp.bfloat16)
        coarse = add_coarse(gather_rows(primal, ("gx", "gy")))
        spread = spread_of(softened, coarse, slots_block, deluxe_panel)
        if schur_partner is not None:
            return spread.astype(jnp.float32) + face_pairs(spread).astype(jnp.float32), schur_partner
        received = jnp.stack(
            [
                from_partner(jnp.concatenate([spread[face], schur_panel[face]]), axis, from_lower)
                for axis, from_lower, face in PARTNERS
            ]
        )
        rows = spread.shape[1]
        spread_partner = received[:, :rows]
        return spread.astype(jnp.float32) + spread_partner.astype(jnp.float32), received[:, rows:]

    def apply_operator(field, schur_partner):
        field_half = field.astype(jnp.bfloat16)
        bent_own = to_half(face_mul(field_half, schur_panel))
        bent_partner = to_half(face_mul(field_half, schur_partner))
        return bent_own + bent_partner

    resid0 = loads_here.astype(jnp.float32) + face_pairs(loads_here).astype(jnp.float32)
    first, schur_partner = precondition(resid0, None)
    resid1 = resid0 - apply_operator(first, schur_partner)
    second, _ = precondition(resid1, schur_partner)
    curved = apply_operator(second, schur_partner)
    partial = jnp.stack(
        [jnp.sum(resid1 * second, axis=(0, 2)), jnp.sum(second * curved, axis=(0, 2))]
    )
    top, bottom = sum_over(partial, ("gx", "gy"))
    step_len = top / bottom
    result = (first + step_len[:, None] * second).astype(jnp.bfloat16)
    return result[None, None]


def solution(mesh):
    return jax.shard_map(
        per_device,
        mesh=mesh,
        in_specs=(
            P("gx", "gy", None, None, None),
            P("gx", "gy", None, None, None),
            P("gx", "gy", None, None, None),
            P("gx", "gy", None, None, None),
            P(("gx", "gy"), None),
            P("gx", "gy", None),
            P("gx", "gy", None),
        ),
        out_specs=P("gx", "gy", None, None, None),
        check_vma=False,
    )
```

```python
import jax
import jax.numpy as jnp
from jax import lax
from jax.experimental import pallas as pl
from jax.sharding import PartitionSpec as P


def with_halo(block, sides, width):
    for axis, dim in sides:
        count = lax.axis_size(axis)
        forward = [(i, i + 1) for i in range(count - 1)]
        backward = [(target, source) for source, target in forward]
        low = lax.ppermute(
            lax.slice_in_dim(block, block.shape[dim] - width, None, axis=dim), axis, forward
        )
        high = lax.ppermute(lax.slice_in_dim(block, 0, width, axis=dim), axis, backward)
        block = jnp.concatenate([low, block, high], axis=dim)
    return block


def gather_rows(block, axes):
    count = lax.axis_size(axes)
    spread = jnp.broadcast_to(block[None], (count,) + block.shape)
    swapped = lax.all_to_all(spread, axes, 0, 0, tiled=False)
    return swapped.reshape((count * block.shape[0],) + block.shape[1:])


def sum_over(block, axes):
    return jnp.sum(gather_rows(block[None], axes), axis=0)


PARTNERS = (("gx", True, 1), ("gx", False, 0), ("gy", True, 3), ("gy", False, 2))


def from_partner(values, axis, from_lower):
    count = lax.axis_size(axis)
    if from_lower:
        pairs = [(i, i + 1) for i in range(count - 1)]
    else:
        pairs = [(i + 1, i) for i in range(count - 1)]
    return lax.ppermute(values, axis, pairs)


def to_half(values):
    return lax.reduce_precision(values, exponent_bits=8, mantissa_bits=7)


def face_mul(vectors, matrices):
    return jnp.einsum("fry,fyx->frx", vectors, matrices, preferred_element_type=jnp.float32)


def face_mul_turned(vectors, matrices):
    return jnp.einsum("fry,fxy->frx", vectors, matrices, preferred_element_type=jnp.float32)


def soften_kernel(scaled_ref, panels_ref, flags_ref, out_ref):
    local_part = jnp.dot(scaled_ref[0], panels_ref[0], preferred_element_type=jnp.float32)
    extra = jnp.dot(
        local_part.astype(jnp.bfloat16), panels_ref[0], preferred_element_type=jnp.float32
    )
    out_ref[0] = local_part + flags_ref[0, 0:1, 0:1] * extra


def soften(scaled, panels, half_flags):
    faces, rows, width = scaled.shape
    flags = jnp.broadcast_to(half_flags[:, None, None], (faces, 8, 128))
    return pl.pallas_call(
        soften_kernel,
        grid=(faces,),
        in_specs=[
            pl.BlockSpec((1, rows, width), lambda f: (f, 0, 0)),
            pl.BlockSpec((1, width, width), lambda f: (f, 0, 0)),
            pl.BlockSpec((1, 8, 128), lambda f: (f, 0, 0)),
        ],
        out_specs=pl.BlockSpec((1, rows, width), lambda f: (f, 0, 0)),
        out_shape=jax.ShapeDtypeStruct((faces, rows, width), jnp.float32),
        cost_estimate=pl.CostEstimate(
            flops=4 * faces * rows * width * width,
            transcendentals=0,
            bytes_accessed=faces * (rows * width * 6 + width * width * 2),
        ),
    )(scaled, panels, flags)


def spread_kernel(softened_ref, coarse_ref, slots_ref, deluxe_ref, out_ref):
    faces, rows, width = softened_ref.shape
    for face in range(faces):
        position = lax.broadcasted_iota(jnp.int32, (1, width), 1) + face * width
        placed = jnp.zeros((rows, width), jnp.float32)
        for k in range(coarse_ref.shape[1]):
            hit = slots_ref[0:1, k:k + 1] == position
            placed = placed + jnp.where(hit, coarse_ref[:, k:k + 1], 0.0)
        weighted = (softened_ref[face] + placed).astype(jnp.bfloat16)
        out_ref[face] = jnp.dot(
            weighted, deluxe_ref[face], preferred_element_type=jnp.float32
        ).astype(out_ref.dtype)


def spread_of(softened, coarse, slots_block, deluxe):
    faces, rows, width = softened.shape
    count = coarse.shape[0]
    return pl.pallas_call(
        spread_kernel,
        out_shape=jax.ShapeDtypeStruct((faces, rows, width), jnp.bfloat16),
        cost_estimate=pl.CostEstimate(
            flops=2 * faces * rows * width * width,
            transcendentals=0,
            bytes_accessed=faces * (rows * width * 6 + width * width * 2),
        ),
    )(softened, coarse.T, slots_block, deluxe)


def face_pairs(values):
    along_first = with_halo(values[0:2], (("gx", 0),), 1)
    along_second = with_halo(values[2:4], (("gy", 0),), 1)
    return jnp.stack([along_first[0], along_first[3], along_second[0], along_second[3]], axis=0)


def per_device(load_parts, schur, deluxe, panels, coarse_inverse, primal_dofs, damage_flags):
    loads_here = load_parts[0, 0]
    schur_panel = schur[0, 0]
    deluxe_panel = deluxe[0, 0]
    inverse_panel = panels[0, 0]
    primal_slots = primal_dofs[0, 0]
    flag_values = damage_flags[0, 0]
    width = loads_here.shape[2]
    primal_count = primal_slots.shape[0]
    positions = jnp.arange(4 * width, dtype=jnp.int32)
    picks = (primal_slots[:, None] == positions[None, :]).reshape(primal_count, 4, width)
    picks_half = picks.astype(jnp.bfloat16)
    slots_block = jnp.zeros((8, 128), jnp.int32).at[0, :primal_count].set(primal_slots)
    flags_full = flag_values.astype(jnp.float32)

    def add_coarse(piece):
        return jnp.dot(coarse_inverse, piece.astype(jnp.float32), precision=lax.Precision.HIGHEST)

    def precondition(resid, schur_partner):
        scaled = face_mul_turned(resid.astype(jnp.bfloat16), deluxe_panel).astype(jnp.bfloat16)
        softened = soften(scaled, inverse_panel, 0.5 * flags_full)
        primal = jnp.einsum(
            "kfx,frx->kr", picks_half, scaled, preferred_element_type=jnp.float32
        ).astype(jnp.bfloat16)
        coarse = add_coarse(gather_rows(primal, ("gx", "gy")))
        spread = spread_of(softened, coarse, slots_block, deluxe_panel)
        if schur_partner is not None:
            return spread.astype(jnp.float32) + face_pairs(spread).astype(jnp.float32), schur_partner
        received = jnp.stack(
            [
                from_partner(jnp.concatenate([spread[face], schur_panel[face]]), axis, from_lower)
                for axis, from_lower, face in PARTNERS
            ]
        )
        rows = spread.shape[1]
        spread_partner = received[:, :rows]
        return spread.astype(jnp.float32) + spread_partner.astype(jnp.float32), received[:, rows:]

    def apply_operator(field, schur_partner):
        field_half = field.astype(jnp.bfloat16)
        bent_own = to_half(face_mul(field_half, schur_panel))
        bent_partner = to_half(face_mul(field_half, schur_partner))
        return bent_own + bent_partner

    resid0 = loads_here.astype(jnp.float32) + face_pairs(loads_here).astype(jnp.float32)
    first, schur_partner = precondition(resid0, None)
    resid1 = resid0 - apply_operator(first, schur_partner)
    second, _ = precondition(resid1, schur_partner)
    curved = apply_operator(second, schur_partner)
    partial = jnp.stack(
        [jnp.sum(resid1 * second, axis=(0, 2)), jnp.sum(second * curved, axis=(0, 2))]
    )
    top, bottom = sum_over(partial, ("gx", "gy"))
    step_len = top / bottom
    result = (first + step_len[:, None] * second).astype(jnp.bfloat16)
    return result[None, None]


def solution(mesh):
    return jax.shard_map(
        per_device,
        mesh=mesh,
        in_specs=(
            P("gx", "gy", None, None, None),
            P("gx", "gy", None, None, None),
            P("gx", "gy", None, None, None),
            P("gx", "gy", None, None, None),
            P(("gx", "gy"), None),
            P("gx", "gy", None),
            P("gx", "gy", None),
        ),
        out_specs=P("gx", "gy", None, None, None),
        check_vma=False,
    )
```

```python
import jax
import jax.numpy as jnp
from jax import lax
from jax.experimental import pallas as pl
from jax.sharding import PartitionSpec as P


def with_halo(block, sides, width):
    for axis, dim in sides:
        count = lax.axis_size(axis)
        forward = [(i, i + 1) for i in range(count - 1)]
        backward = [(target, source) for source, target in forward]
        low = lax.ppermute(
            lax.slice_in_dim(block, block.shape[dim] - width, None, axis=dim), axis, forward
        )
        high = lax.ppermute(lax.slice_in_dim(block, 0, width, axis=dim), axis, backward)
        block = jnp.concatenate([low, block, high], axis=dim)
    return block


def gather_rows(block, axes):
    count = lax.axis_size(axes)
    spread = jnp.broadcast_to(block[None], (count,) + block.shape)
    swapped = lax.all_to_all(spread, axes, 0, 0, tiled=False)
    return swapped.reshape((count * block.shape[0],) + block.shape[1:])


def sum_over(block, axes):
    return jnp.sum(gather_rows(block[None], axes), axis=0)


PARTNERS = (("gx", True, 1), ("gx", False, 0), ("gy", True, 3), ("gy", False, 2))


def from_partner(values, axis, from_lower):
    count = lax.axis_size(axis)
    if from_lower:
        pairs = [(i, i + 1) for i in range(count - 1)]
    else:
        pairs = [(i + 1, i) for i in range(count - 1)]
    return lax.ppermute(values, axis, pairs)


def to_half(values):
    return lax.reduce_precision(values, exponent_bits=8, mantissa_bits=7)


def face_mul(vectors, matrices):
    return jnp.einsum("fry,fyx->frx", vectors, matrices, preferred_element_type=jnp.float32)


def face_mul_turned(vectors, matrices):
    return jnp.einsum("fry,fxy->frx", vectors, matrices, preferred_element_type=jnp.float32)


def soften_kernel(scaled_ref, panels_ref, flags_ref, out_ref):
    local_part = jnp.dot(scaled_ref[0], panels_ref[0], preferred_element_type=jnp.float32)
    extra = jnp.dot(
        local_part.astype(jnp.bfloat16), panels_ref[0], preferred_element_type=jnp.float32
    )
    out_ref[0] = local_part + flags_ref[0, 0:1, 0:1] * extra


def soften(scaled, panels, half_flags):
    faces, rows, width = scaled.shape
    flags = jnp.broadcast_to(half_flags[:, None, None], (faces, 8, 128))
    return pl.pallas_call(
        soften_kernel,
        grid=(faces,),
        in_specs=[
            pl.BlockSpec((1, rows, width), lambda f: (f, 0, 0)),
            pl.BlockSpec((1, width, width), lambda f: (f, 0, 0)),
            pl.BlockSpec((1, 8, 128), lambda f: (f, 0, 0)),
        ],
        out_specs=pl.BlockSpec((1, rows, width), lambda f: (f, 0, 0)),
        out_shape=jax.ShapeDtypeStruct((faces, rows, width), jnp.float32),
        cost_estimate=pl.CostEstimate(
            flops=4 * faces * rows * width * width,
            transcendentals=0,
            bytes_accessed=faces * (rows * width * 6 + width * width * 2),
        ),
    )(scaled, panels, flags)


def face_pairs(values):
    along_first = with_halo(values[0:2], (("gx", 0),), 1)
    along_second = with_halo(values[2:4], (("gy", 0),), 1)
    return jnp.stack([along_first[0], along_first[3], along_second[0], along_second[3]], axis=0)


def per_device(load_parts, schur, deluxe, panels, coarse_inverse, primal_dofs, damage_flags):
    loads_here = load_parts[0, 0]
    schur_panel = schur[0, 0]
    deluxe_panel = deluxe[0, 0]
    inverse_panel = panels[0, 0]
    primal_slots = primal_dofs[0, 0]
    flag_values = damage_flags[0, 0]
    width = loads_here.shape[2]
    primal_count = primal_slots.shape[0]
    positions = jnp.arange(4 * width, dtype=jnp.int32)
    picks = (primal_slots[:, None] == positions[None, :]).reshape(primal_count, 4, width)
    picks_half = picks.astype(jnp.bfloat16)
    flags_full = flag_values.astype(jnp.float32)

    def add_coarse(piece):
        return jnp.dot(coarse_inverse, piece.astype(jnp.float32), precision=lax.Precision.HIGHEST)

    def precondition(resid, schur_partner):
        scaled = face_mul_turned(resid.astype(jnp.bfloat16), deluxe_panel).astype(jnp.bfloat16)
        softened = soften(scaled, inverse_panel, 0.5 * flags_full)
        primal = jnp.einsum(
            "kfx,frx->kr", picks_half, scaled, preferred_element_type=jnp.float32
        ).astype(jnp.bfloat16)
        coarse = add_coarse(gather_rows(primal, ("gx", "gy")))
        placed = jnp.zeros_like(softened)
        for k in range(primal_count):
            placed = placed + jnp.where(picks[k][:, None, :], coarse[k][None, :, None], 0.0)
        weighted = (softened + placed).astype(jnp.bfloat16)
        spread = face_mul(weighted, deluxe_panel).astype(jnp.bfloat16)
        if schur_partner is not None:
            return spread.astype(jnp.float32) + face_pairs(spread).astype(jnp.float32), schur_partner
        received = jnp.stack(
            [
                from_partner(jnp.concatenate([spread[face], schur_panel[face]]), axis, from_lower)
                for axis, from_lower, face in PARTNERS
            ]
        )
        rows = spread.shape[1]
        spread_partner = received[:, :rows]
        return spread.astype(jnp.float32) + spread_partner.astype(jnp.float32), received[:, rows:]

    def apply_operator(field, schur_partner):
        field_half = field.astype(jnp.bfloat16)
        bent_own = to_half(face_mul(field_half, schur_panel))
        bent_partner = to_half(face_mul(field_half, schur_partner))
        return bent_own + bent_partner

    resid0 = loads_here.astype(jnp.float32) + face_pairs(loads_here).astype(jnp.float32)
    first, schur_partner = precondition(resid0, None)
    resid1 = resid0 - apply_operator(first, schur_partner)
    second, _ = precondition(resid1, schur_partner)
    curved = apply_operator(second, schur_partner)
    partial = jnp.stack(
        [jnp.sum(resid1 * second, axis=(0, 2)), jnp.sum(second * curved, axis=(0, 2))]
    )
    top, bottom = sum_over(partial, ("gx", "gy"))
    step_len = top / bottom
    result = (first + step_len[:, None] * second).astype(jnp.bfloat16)
    return result[None, None]


def solution(mesh):
    return jax.shard_map(
        per_device,
        mesh=mesh,
        in_specs=(
            P("gx", "gy", None, None, None),
            P("gx", "gy", None, None, None),
            P("gx", "gy", None, None, None),
            P("gx", "gy", None, None, None),
            P(("gx", "gy"), None),
            P("gx", "gy", None),
            P("gx", "gy", None),
        ),
        out_specs=P("gx", "gy", None, None, None),
        check_vma=False,
    )
```

```python
import jax
import jax.numpy as jnp
from jax import lax
from jax.experimental import pallas as pl
from jax.sharding import PartitionSpec as P


def with_halo(block, sides, width):
    for axis, dim in sides:
        count = lax.axis_size(axis)
        forward = [(i, i + 1) for i in range(count - 1)]
        backward = [(target, source) for source, target in forward]
        low = lax.ppermute(
            lax.slice_in_dim(block, block.shape[dim] - width, None, axis=dim), axis, forward
        )
        high = lax.ppermute(lax.slice_in_dim(block, 0, width, axis=dim), axis, backward)
        block = jnp.concatenate([low, block, high], axis=dim)
    return block


def gather_rows(block, axes):
    count = lax.axis_size(axes)
    spread = jnp.broadcast_to(block[None], (count,) + block.shape)
    swapped = lax.all_to_all(spread, axes, 0, 0, tiled=False)
    return swapped.reshape((count * block.shape[0],) + block.shape[1:])


def sum_over(block, axes):
    return jnp.sum(gather_rows(block[None], axes), axis=0)


PARTNERS = (("gx", True, 1), ("gx", False, 0), ("gy", True, 3), ("gy", False, 2))


def from_partner(values, axis, from_lower):
    count = lax.axis_size(axis)
    if from_lower:
        pairs = [(i, i + 1) for i in range(count - 1)]
    else:
        pairs = [(i + 1, i) for i in range(count - 1)]
    return lax.ppermute(values, axis, pairs)


def to_half(values):
    return lax.reduce_precision(values, exponent_bits=8, mantissa_bits=7)


def face_mul(vectors, matrices):
    return jnp.einsum("fry,fyx->frx", vectors, matrices, preferred_element_type=jnp.float32)


def face_mul_turned(vectors, matrices):
    return jnp.einsum("fry,fxy->frx", vectors, matrices, preferred_element_type=jnp.float32)


def soften_kernel(scaled_ref, panels_ref, flags_ref, out_ref):
    local_part = jnp.dot(scaled_ref[0], panels_ref[0], preferred_element_type=jnp.float32)
    extra = jnp.dot(
        local_part.astype(jnp.bfloat16), panels_ref[0], preferred_element_type=jnp.float32
    )
    out_ref[0] = local_part + flags_ref[0, 0:1, 0:1] * extra


def soften(scaled, panels, half_flags):
    faces, rows, width = scaled.shape
    flags = jnp.broadcast_to(half_flags[:, None, None], (faces, 8, 128))
    return pl.pallas_call(
        soften_kernel,
        grid=(faces,),
        in_specs=[
            pl.BlockSpec((1, rows, width), lambda f: (f, 0, 0)),
            pl.BlockSpec((1, width, width), lambda f: (f, 0, 0)),
            pl.BlockSpec((1, 8, 128), lambda f: (f, 0, 0)),
        ],
        out_specs=pl.BlockSpec((1, rows, width), lambda f: (f, 0, 0)),
        out_shape=jax.ShapeDtypeStruct((faces, rows, width), jnp.float32),
        cost_estimate=pl.CostEstimate(
            flops=4 * faces * rows * width * width,
            transcendentals=0,
            bytes_accessed=faces * (rows * width * 6 + width * width * 2),
        ),
    )(scaled, panels, flags)


def face_pairs(values):
    along_first = with_halo(values[0:2], (("gx", 0),), 1)
    along_second = with_halo(values[2:4], (("gy", 0),), 1)
    return jnp.stack([along_first[0], along_first[3], along_second[0], along_second[3]], axis=0)


def per_device(load_parts, schur, deluxe, panels, coarse_inverse, primal_dofs, damage_flags):
    loads_here = load_parts[0, 0]
    schur_panel = schur[0, 0]
    deluxe_panel = deluxe[0, 0]
    inverse_panel = panels[0, 0]
    primal_slots = primal_dofs[0, 0]
    flag_values = damage_flags[0, 0]
    width = loads_here.shape[2]
    primal_count = primal_slots.shape[0]
    positions = jnp.arange(4 * width, dtype=jnp.int32)
    picks = (primal_slots[:, None] == positions[None, :]).reshape(primal_count, 4, width)
    picks_half = picks.astype(jnp.bfloat16)
    flags_full = flag_values.astype(jnp.float32)

    def add_coarse(piece):
        return jnp.dot(coarse_inverse, piece.astype(jnp.float32), precision=lax.Precision.HIGHEST)

    def precondition(resid, schur_partner):
        scaled = face_mul_turned(resid.astype(jnp.bfloat16), deluxe_panel).astype(jnp.bfloat16)
        softened = soften(scaled, inverse_panel, 0.5 * flags_full)
        primal = jnp.einsum(
            "kfx,frx->kr", picks_half, scaled, preferred_element_type=jnp.float32
        ).astype(jnp.bfloat16)
        coarse = add_coarse(gather_rows(primal, ("gx", "gy")))
        faces = softened.shape[0]
        position = lax.broadcasted_iota(jnp.int32, softened.shape, 0) * width + lax.broadcasted_iota(
            jnp.int32, softened.shape, 2
        )
        placed = jnp.zeros_like(softened)
        for k in range(primal_count):
            placed = placed + jnp.where(position == primal_slots[k], coarse[k][None, :, None], 0.0)
        weighted = (softened + placed).astype(jnp.bfloat16)
        spread = face_mul(weighted, deluxe_panel).astype(jnp.bfloat16)
        if schur_partner is not None:
            return spread.astype(jnp.float32) + face_pairs(spread).astype(jnp.float32), schur_partner
        received = jnp.stack(
            [
                from_partner(jnp.concatenate([spread[face], schur_panel[face]]), axis, from_lower)
                for axis, from_lower, face in PARTNERS
            ]
        )
        rows = spread.shape[1]
        spread_partner = received[:, :rows]
        return spread.astype(jnp.float32) + spread_partner.astype(jnp.float32), received[:, rows:]

    def apply_operator(field, schur_partner):
        field_half = field.astype(jnp.bfloat16)
        bent_own = to_half(face_mul(field_half, schur_panel))
        bent_partner = to_half(face_mul(field_half, schur_partner))
        return bent_own + bent_partner

    resid0 = loads_here.astype(jnp.float32) + face_pairs(loads_here).astype(jnp.float32)
    first, schur_partner = precondition(resid0, None)
    resid1 = resid0 - apply_operator(first, schur_partner)
    second, _ = precondition(resid1, schur_partner)
    curved = apply_operator(second, schur_partner)
    partial = jnp.stack(
        [jnp.sum(resid1 * second, axis=(0, 2)), jnp.sum(second * curved, axis=(0, 2))]
    )
    top, bottom = sum_over(partial, ("gx", "gy"))
    step_len = top / bottom
    result = (first + step_len[:, None] * second).astype(jnp.bfloat16)
    return result[None, None]


def solution(mesh):
    return jax.shard_map(
        per_device,
        mesh=mesh,
        in_specs=(
            P("gx", "gy", None, None, None),
            P("gx", "gy", None, None, None),
            P("gx", "gy", None, None, None),
            P("gx", "gy", None, None, None),
            P(("gx", "gy"), None),
            P("gx", "gy", None),
            P("gx", "gy", None),
        ),
        out_specs=P("gx", "gy", None, None, None),
        check_vma=False,
    )
```
